512 devices in a mesh: seq: 128 (over z, y, core), head: 4 (over x).
Axes of the slice: x: 4, y: 8, z: 8, core: 2. Of those that a mesh axis runs over, the one named last changes fastest.
Arguments:
- tokens: bfloat16 [16384, 4096], P('seq', 'head'), may hold values from -120 to 120
- shared_weight: bfloat16 [4096, 512], P(None, 'head'), may hold values from -0.75 to 0.75
- value_weight: bfloat16 [4096, 512], P(None, 'head'), may hold values from -0.09375 to 0.09375
- head_grad: bfloat16 [16384, 512], P('seq', 'head'), may hold values from -0.75 to 0.75
- sorted_slot: int32 [4, 16384], P('head', 'seq'), may hold values from 0 to 16383, as said below
Outputs:
- shared_grad: float32 [4096, 512], P('seq', 'head')
- value_grad: float32 [4096, 512], P('seq', 'head')
The draws below stay inside these ranges and needn't reach their ends.
Inputs may be any that keep to these rules, and one draw needn't show every extreme that they name: For each head, sorted_slot[h] is a permutation of the positions. Of the 128 positions of one device (positions r * 128 to (r+1) * 128 - 1), at most 2 have sorted indices in the range s * 128 to (s+1) * 128 - 1 of one device s, for every head, and in every head some pair r, s reaches 2.
All inputs are finite; a program needn't handle non-finite values.
Results may differ from the reference program's by a relative error of at most 0.006.
The reference program's roundings to bfloat16 on the way count: a program that leaves them out, or rounds other values in their place, can miss the bound.
Values may be sent and summed in bfloat16 or wider, within the bound.
No kernel may reach another device: no remote copies, remote signals or barrier semaphores. Data moves between devices by JAX's collectives and lax.ppermute only.
A program may use at most 64 MiB of HBM per device.

```python
import math
import jax
import jax.numpy as jnp
from jax import lax

D = 4096
DH = 128
GROUP = 64
TOK_DEV = 128
HEADS = 4
SEQ = 16384
N_SEQ = 128


def slot_table(base_key):
    mean_count = TOK_DEV // N_SEQ

    def one_head(head_key):
        keys_list = jax.random.split(head_key, 5)
        pairing = jax.random.permutation(keys_list[0], N_SEQ)
        swing = jax.random.randint(keys_list[1], (N_SEQ // 2,), -mean_count, mean_count + 1)
        swing = swing.at[0].set(mean_count)
        counts = jnp.zeros((N_SEQ,), jnp.int32).at[pairing[0::2]].set(mean_count + swing)
        counts = counts.at[pairing[1::2]].set(mean_count - swing)
        running = jnp.cumsum(counts)
        offsets = jnp.searchsorted(running, jnp.arange(TOK_DEV, dtype=jnp.int32), side='right').astype(jnp.int32)
        offsets = offsets[jax.random.permutation(keys_list[2], TOK_DEV)]
        layer_ids = jnp.arange(TOK_DEV, dtype=jnp.int32)[None, :]
        score_owner = jax.random.randint(keys_list[3], (N_SEQ, TOK_DEV), 0, TOK_DEV) * TOK_DEV + layer_ids
        score_target = jax.random.randint(keys_list[4], (N_SEQ, TOK_DEV), 0, TOK_DEV) * TOK_DEV + layer_ids
        owner_order = jnp.argsort(score_owner, axis=1, stable=True).astype(jnp.int32)
        target_order = jnp.argsort(score_target, axis=1, stable=True).astype(jnp.int32)
        owners = jnp.arange(N_SEQ, dtype=jnp.int32)[:, None]
        position = owners * TOK_DEV + owner_order
        targets = (owners - offsets[None, :]) % N_SEQ
        layer_grid = jnp.broadcast_to(layer_ids, (N_SEQ, TOK_DEV))
        slot_value = targets * TOK_DEV + target_order[targets, layer_grid]
        return jnp.zeros((SEQ,), jnp.int32).at[position.reshape(-1)].set(slot_value.reshape(-1))
    head_keys = jax.random.split(jax.random.fold_in(base_key, 11), HEADS)
    return jax.vmap(one_head)(head_keys)


def draw_sorted_slot(key, part):
    return slot_table(key)


def draw_tokens(key, part):
    slots = slot_table(key)
    keys_list = jax.random.split(jax.random.fold_in(key, 23), 5)
    base = jnp.clip(jax.random.normal(keys_list[0], (SEQ, D), jnp.float32), -6.0, 6.0)
    pairing = jax.random.permutation(keys_list[2], N_SEQ)
    row_block = jnp.arange(SEQ, dtype=jnp.int32) // TOK_DEV
    col_block = jnp.arange(D, dtype=jnp.int32) // (D // N_SEQ)
    boost = jnp.where(pairing[row_block][:, None] == col_block[None, :], 4.0, 1.0)
    base = base * boost
    positions = jnp.arange(SEQ, dtype=jnp.int32)
    order = jax.vmap(lambda row: jnp.zeros((SEQ,), jnp.int32).at[row].set(positions))(slots)
    strength = jnp.array([16.0, 22.0, 28.0], jnp.float32)
    spread = jnp.sqrt(0.5 / strength)
    shape_hot = (HEADS, 3, D)
    common = jnp.clip(jax.random.normal(keys_list[3], shape_hot, jnp.float32), -4.0, 4.0)
    other = jnp.clip(jax.random.normal(keys_list[4], shape_hot, jnp.float32), -4.0, 4.0)
    row_query = strength[None, :, None] * common
    row_first = 2.0 * common
    row_second = 3.0 * (common + spread[None, :, None] * other)
    head_ids = jnp.arange(HEADS, dtype=jnp.int32)[:, None]
    triple_ids = jnp.arange(3, dtype=jnp.int32)[None, :]
    device_ids = (triple_ids * HEADS + head_ids) % N_SEQ
    start_slot = device_ids * TOK_DEV + 3
    head_grid = jnp.broadcast_to(head_ids, (HEADS, 3))
    pos_query = order[head_grid, start_slot]
    pos_first = order[head_grid, start_slot + 1]
    pos_second = order[head_grid, start_slot + 2]
    hot_index = jnp.concatenate([pos_query.reshape(-1), pos_first.reshape(-1), pos_second.reshape(-1)])
    hot_rows = jnp.concatenate([row_query.reshape(-1, D), row_first.reshape(-1, D), row_second.reshape(-1, D)], axis=0)
    tokens = base.at[hot_index].set(hot_rows)
    return jnp.clip(tokens, -120.0, 120.0).astype(jnp.bfloat16)


def shard_levels(rng, extent, cuts, low, high):
    level, own = 1.0, jax.random.fold_in(rng, 6)
    for dim, blocks in cuts:
        heights = jnp.exp(jax.random.uniform(jax.random.fold_in(own, dim), (blocks,), jnp.float32, low / len(cuts), high / len(cuts)))
        level = level * jnp.repeat(heights, extent[dim] // blocks).reshape([-1 if axis == dim else 1 for axis in range(len(extent))])
    return level


def scatter_about(stream_key, shape, scale, bound, pieces=(), held_as=jnp.bfloat16):
    gain = shard_levels(stream_key, shape, pieces, -0.22, 0.18) if pieces else 1.0
    entries = jax.random.normal(stream_key, shape, jnp.float32) * scale * gain
    return jnp.minimum(jnp.maximum(entries, -bound), bound).astype(held_as)


def setup_inputs(seed: int = 0) -> dict:
    streams_of = jax.random.split(jax.random.key(seed), 6)
    tokens = draw_tokens(jax.random.fold_in(streams_of[5], 71), 0)
    shared_weight = scatter_about(streams_of[1], (D, HEADS * DH), (D // 64) ** -0.5, 0.75, ((1, 4),))
    value_weight = scatter_about(streams_of[2], (D, HEADS * DH), D ** -0.5, 0.09375, ((1, 4),))
    head_grad = scatter_about(streams_of[3], (SEQ, HEADS * DH), 0.05, 0.75, ((0, 128), (1, 4)))
    sorted_slot = draw_sorted_slot(jax.random.fold_in(streams_of[5], 71), 0)
    return dict(tokens=tokens, shared_weight=shared_weight, value_weight=value_weight, head_grad=head_grad, sorted_slot=sorted_slot)


eps_norm = 1e-06
masked_score = -1000000000.0

def attend_head(query_sorted, value_sorted, grad_sorted):
    group_count = SEQ // GROUP
    scale_factor = 1.0 / math.sqrt(DH)
    query_float = query_sorted.astype(jnp.float32)
    norm_sorted = jnp.sqrt(lax.optimization_barrier(jnp.sum(query_float * query_float, axis=1, keepdims=True)) + eps_norm)
    key_sorted = (query_float / norm_sorted).astype(jnp.bfloat16)
    q_blocks = query_sorted.reshape(group_count, GROUP, DH).astype(jnp.float32)
    k_blocks = key_sorted.reshape(group_count, GROUP, DH).astype(jnp.float32)
    v_blocks = value_sorted.reshape(group_count, GROUP, DH).astype(jnp.float32)
    g_blocks = grad_sorted.reshape(group_count, GROUP, DH).astype(jnp.float32)
    key_window = jnp.concatenate([k_blocks, jnp.roll(k_blocks, 1, axis=0)], axis=1)
    value_window = jnp.concatenate([v_blocks, jnp.roll(v_blocks, 1, axis=0)], axis=1)
    scores = jnp.einsum('cqd,ckd->cqk', q_blocks, key_window) * scale_factor
    self_mask = jnp.arange(GROUP)[:, None] == jnp.arange(2 * GROUP)[None, :]
    scores = jnp.where(self_mask[None], masked_score, scores)
    probs = jax.nn.softmax(scores, axis=-1)
    dprob = jnp.einsum('cqd,ckd->cqk', g_blocks, value_window)
    dscore = probs * (dprob - lax.optimization_barrier(jnp.sum(probs * dprob, axis=-1, keepdims=True)))
    probs_low = lax.optimization_barrier(probs.astype(jnp.bfloat16)).astype(jnp.float32)
    dscore_low = lax.optimization_barrier(dscore.astype(jnp.bfloat16)).astype(jnp.float32)
    dquery = jnp.einsum('cqk,ckd->cqd', dscore_low, key_window) * scale_factor
    dkey_window = jnp.einsum('cqk,cqd->ckd', dscore_low, q_blocks) * scale_factor
    dvalue_window = jnp.einsum('cqk,cqd->ckd', probs_low, g_blocks)
    dkey = dkey_window[:, :GROUP] + jnp.roll(dkey_window[:, GROUP:], -1, axis=0)
    dvalue = dvalue_window[:, :GROUP] + jnp.roll(dvalue_window[:, GROUP:], -1, axis=0)
    return (dquery.reshape(SEQ, DH), dkey.reshape(SEQ, DH), dvalue.reshape(SEQ, DH))

def reference(tokens, shared_weight, value_weight, head_grad, sorted_slot):
    positions = jnp.arange(SEQ, dtype=jnp.int32)
    shared_parts = []
    value_parts = []
    for head_idx in range(HEADS):
        first_col = head_idx * DH
        query = jnp.dot(tokens, shared_weight[:, first_col:first_col + DH], preferred_element_type=jnp.float32).astype(jnp.bfloat16)
        values = jnp.dot(tokens, value_weight[:, first_col:first_col + DH], preferred_element_type=jnp.float32).astype(jnp.bfloat16)
        grad_head = head_grad[:, first_col:first_col + DH]
        slot_ids = sorted_slot[head_idx].astype(jnp.int32)
        order = jnp.zeros((SEQ,), jnp.int32).at[slot_ids].set(positions)
        dquery_s, dkey_s, dvalue_s = attend_head(query[order], values[order], grad_head[order])
        dquery_p = dquery_s[slot_ids]
        dkey_p = dkey_s[slot_ids]
        dvalue_p = dvalue_s[slot_ids]
        query_float = query.astype(jnp.float32)
        norm_pos = jnp.sqrt(lax.optimization_barrier(jnp.sum(query_float * query_float, axis=1, keepdims=True)) + eps_norm)
        along = lax.optimization_barrier(jnp.sum(query_float * dkey_p, axis=1, keepdims=True))
        dshared = dquery_p + dkey_p / norm_pos - query_float * (along / norm_pos ** 3)
        shared_parts.append(jnp.dot(tokens.T, dshared.astype(jnp.bfloat16), preferred_element_type=jnp.float32))
        value_parts.append(jnp.dot(tokens.T, dvalue_p.astype(jnp.bfloat16), preferred_element_type=jnp.float32))
    return (jnp.concatenate(shared_parts, axis=1), jnp.concatenate(value_parts, axis=1))
```

```python
import math

import jax
import jax.numpy as jnp
from jax import lax
from jax.sharding import Mesh
from jax.sharding import PartitionSpec as P

GROUP = 64

SEQ = ("z", "y", "c")


eps_norm = 1e-06
masked_score = -1000000000.0


def shifted(value, axis, steps):
    count = lax.axis_size(axis)
    pairs = [(source, (source + steps) % count) for source in range(count)]
    return lax.ppermute(value, axis, pairs)


def unit_keys(block):
    block_float = block.astype(jnp.float32)
    norm_rows = jnp.sqrt(jnp.sum(block_float * block_float, axis=1, keepdims=True) + eps_norm)
    return (block_float / norm_rows).astype(jnp.bfloat16)


def per_device(tokens, shared_weight, value_weight, head_grad, sorted_slot):
    whole = lax.all_gather(tokens, "head", axis=1, tiled=True)
    tok_count = whole.shape[0]
    feat_count = whole.shape[1]
    head_width = shared_weight.shape[1]
    peer_count = lax.axis_size(SEQ)
    capacity = 2 * tok_count // peer_count
    group_count = tok_count // GROUP
    tail_start = tok_count - GROUP
    scale_factor = 1.0 / math.sqrt(head_width)
    query = jnp.dot(whole, shared_weight, preferred_element_type=jnp.float32).astype(jnp.bfloat16)
    values = jnp.dot(whole, value_weight, preferred_element_type=jnp.float32).astype(jnp.bfloat16)
    slot_ids = sorted_slot[0]
    target = slot_ids // tok_count
    local_slot = slot_ids - target * tok_count
    peer_ids = jnp.arange(peer_count, dtype=jnp.int32)
    row_ids = jnp.arange(tok_count, dtype=jnp.int32)
    earlier_rows = (row_ids[:, None] > row_ids[None, :]).astype(jnp.bfloat16)
    every_row = jnp.ones((tok_count,), dtype=bool)
    one_hot = ((target[:, None] == peer_ids[None, :]) & every_row[:, None]).astype(jnp.bfloat16)
    before = jnp.dot(earlier_rows, one_hot, preferred_element_type=jnp.float32)
    buffer_index = target * capacity + jnp.sum(before * one_hot.astype(jnp.float32), axis=1).astype(
        jnp.int32
    )
    payload = jnp.concatenate([query, values, head_grad], axis=1)
    send_rows = (
        jnp.zeros((peer_count * capacity, 3 * head_width), jnp.bfloat16)
        .at[buffer_index]
        .set(payload)
    )
    send_slots = (
        jnp.full((peer_count * capacity,), tok_count, jnp.int32).at[buffer_index].set(local_slot)
    )
    recv_rows, recv_slots = (
        lax.all_to_all(send_rows, SEQ, split_axis=0, concat_axis=0, tiled=True),
        lax.all_to_all(send_slots, SEQ, split_axis=0, concat_axis=0, tiled=True),
    )
    sorted_rows = (
        jnp.zeros((tok_count, 3 * head_width), jnp.bfloat16)
        .at[recv_slots]
        .set(recv_rows, mode="drop")
    )
    halo_rows = shifted(sorted_rows[tail_start:, : 2 * head_width], SEQ, 1)
    sorted_query = sorted_rows[:, :head_width]
    own_keys = unit_keys(sorted_query).reshape(group_count, GROUP, head_width)
    halo_keys = unit_keys(halo_rows[:, :head_width])
    q_blocks = sorted_query.reshape(group_count, GROUP, head_width)
    v_blocks = sorted_rows[:, head_width : 2 * head_width].reshape(group_count, GROUP, head_width)
    g_blocks = sorted_rows[:, 2 * head_width :].reshape(group_count, GROUP, head_width)
    prev_keys = jnp.concatenate([halo_keys[None], own_keys[:-1]], axis=0)
    prev_values = jnp.concatenate([halo_rows[None, :, head_width:], v_blocks[:-1]], axis=0)
    key_window = jnp.concatenate([own_keys, prev_keys], axis=1)
    value_window = jnp.concatenate([v_blocks, prev_values], axis=1)
    scores = (
        jnp.einsum("cqd,ckd->cqk", q_blocks, key_window, preferred_element_type=jnp.float32)
        * scale_factor
    )
    self_mask = jnp.arange(GROUP)[:, None] == jnp.arange(2 * GROUP)[None, :]
    scores = jnp.where(self_mask[None], masked_score, scores)
    probs = jax.nn.softmax(scores, axis=-1)
    dprob = jnp.einsum("cqd,ckd->cqk", g_blocks, value_window, preferred_element_type=jnp.float32)
    dscore = probs * (dprob - jnp.sum(probs * dprob, axis=-1, keepdims=True))
    probs_low = probs.astype(jnp.bfloat16)
    dscore_low = dscore.astype(jnp.bfloat16)
    dquery = (
        jnp.einsum("cqk,ckd->cqd", dscore_low, key_window, preferred_element_type=jnp.float32)
        * scale_factor
    )
    dkey_window = (
        jnp.einsum("cqk,cqd->ckd", dscore_low, q_blocks, preferred_element_type=jnp.float32)
        * scale_factor
    )
    dvalue_window = jnp.einsum(
        "cqk,cqd->ckd", probs_low, g_blocks, preferred_element_type=jnp.float32
    )
    grad_window = jnp.concatenate([dkey_window, dvalue_window], axis=-1)
    own_part = grad_window[:, :GROUP]
    later_part = grad_window[1:, GROUP:]
    outgoing = grad_window[0, GROUP:]
    incoming = shifted(outgoing, SEQ, -1)
    key_value = (own_part + jnp.concatenate([later_part, incoming[None]], axis=0)).reshape(
        tok_count, 2 * head_width
    )
    dquery_s = dquery.reshape(tok_count, head_width)
    dkey_s = key_value[:, :head_width]
    dvalue_s = key_value[:, head_width:]
    query_float = sorted_query.astype(jnp.float32)
    norm_s = jnp.sqrt(jnp.sum(query_float * query_float, axis=1, keepdims=True) + eps_norm)
    along = jnp.sum(query_float * dkey_s, axis=1, keepdims=True)
    dshared_s = dquery_s + dkey_s / norm_s - query_float * (along / norm_s**3)
    sorted_grads = jnp.concatenate(
        [dshared_s.astype(jnp.bfloat16), dvalue_s.astype(jnp.bfloat16)], axis=1
    )
    return_rows = sorted_grads[jnp.minimum(recv_slots, tok_count - 1)]
    back_rows = lax.all_to_all(return_rows, SEQ, split_axis=0, concat_axis=0, tiled=True)
    combined = back_rows[buffer_index]
    nz, ny, nc = (lax.axis_size(a) for a in SEQ)
    blocks = whole.reshape(tok_count, nz, ny, nc, feat_count // (nz * ny * nc))
    partial = jnp.einsum(
        "pzyck,ph->cyzkh", blocks, combined, preferred_element_type=jnp.float32
    ).reshape(feat_count, 2 * head_width)
    grads = partial
    for axis in ("c", "y", "z"):
        grads = lax.psum_scatter(grads, axis, scatter_dimension=0, tiled=True)
    return (grads[:, :head_width], grads[:, head_width:])


def split_mesh(mesh):
    devices = mesh.devices
    seq_n, head_n = devices.shape
    column = devices[:, 0]
    cores = sorted({d.core_on_chip for d in column})
    ys = sorted({d.coords[1] for d in column})
    nc, ny = len(cores), len(ys)
    nz = seq_n // (nc * ny)
    grid = devices.reshape(nz, ny, nc, head_n)
    for z in range(nz):
        for y in range(ny):
            for c in range(nc):
                d = grid[z, y, c, 0]
                assert d.core_on_chip == cores[c] and d.coords[1] == ys[y]
    return Mesh(grid, SEQ + ("head",))


def solution(mesh):
    fine = split_mesh(mesh)
    in_specs = (
        P(SEQ, "head"),
        P(None, "head"),
        P(None, "head"),
        P(SEQ, "head"),
        P("head", SEQ),
    )
    out_specs = (P(SEQ, "head"), P(SEQ, "head"))
    return jax.shard_map(
        per_device, mesh=fine, in_specs=in_specs, out_specs=out_specs, check_vma=False
    )
```

```python
import math

import jax
import jax.numpy as jnp
from jax import lax
from jax.sharding import Mesh
from jax.sharding import PartitionSpec as P

GROUP = 64

SEQ = ("z", "y", "c")


eps_norm = 1e-06
masked_score = -1000000000.0


def shifted(value, axis, steps):
    count = lax.axis_size(axis)
    pairs = [(source, (source + steps) % count) for source in range(count)]
    return lax.ppermute(value, axis, pairs)


def unit_keys(block):
    block_float = block.astype(jnp.float32)
    norm_rows = jnp.sqrt(jnp.sum(block_float * block_float, axis=1, keepdims=True) + eps_norm)
    return (block_float / norm_rows).astype(jnp.bfloat16)


def per_device(tokens, shared_weight, value_weight, head_grad, sorted_slot):
    tok_count = tokens.shape[0]
    head_n = lax.axis_size("head")
    spread = jnp.broadcast_to(tokens[None], (head_n,) + tokens.shape)
    gathered = lax.all_to_all(spread, "head", 0, 0, tiled=True)
    whole = gathered.transpose(1, 0, 2).reshape(tok_count, head_n * tokens.shape[1])
    feat_count = whole.shape[1]
    head_width = shared_weight.shape[1]
    peer_count = lax.axis_size(SEQ)
    capacity = 2 * tok_count // peer_count
    group_count = tok_count // GROUP
    tail_start = tok_count - GROUP
    scale_factor = 1.0 / math.sqrt(head_width)
    query = jnp.dot(whole, shared_weight, preferred_element_type=jnp.float32).astype(jnp.bfloat16)
    values = jnp.dot(whole, value_weight, preferred_element_type=jnp.float32).astype(jnp.bfloat16)
    slot_ids = sorted_slot[0]
    target = slot_ids // tok_count
    local_slot = slot_ids - target * tok_count
    peer_ids = jnp.arange(peer_count, dtype=jnp.int32)
    row_ids = jnp.arange(tok_count, dtype=jnp.int32)
    earlier_rows = (row_ids[:, None] > row_ids[None, :]).astype(jnp.bfloat16)
    every_row = jnp.ones((tok_count,), dtype=bool)
    one_hot = ((target[:, None] == peer_ids[None, :]) & every_row[:, None]).astype(jnp.bfloat16)
    before = jnp.dot(earlier_rows, one_hot, preferred_element_type=jnp.float32)
    buffer_index = target * capacity + jnp.sum(before * one_hot.astype(jnp.float32), axis=1).astype(
        jnp.int32
    )
    payload = jnp.concatenate([query, values, head_grad], axis=1)
    send_rows = (
        jnp.zeros((peer_count * capacity, 3 * head_width), jnp.bfloat16)
        .at[buffer_index]
        .set(payload)
    )
    send_slots = (
        jnp.full((peer_count * capacity,), tok_count, jnp.int32).at[buffer_index].set(local_slot)
    )
    recv_rows, recv_slots = (
        lax.all_to_all(send_rows, SEQ, split_axis=0, concat_axis=0, tiled=True),
        lax.all_to_all(send_slots, SEQ, split_axis=0, concat_axis=0, tiled=True),
    )
    sorted_rows = (
        jnp.zeros((tok_count, 3 * head_width), jnp.bfloat16)
        .at[recv_slots]
        .set(recv_rows, mode="drop")
    )
    halo_rows = shifted(sorted_rows[tail_start:, : 2 * head_width], SEQ, 1)
    sorted_query = sorted_rows[:, :head_width]
    own_keys = unit_keys(sorted_query).reshape(group_count, GROUP, head_width)
    halo_keys = unit_keys(halo_rows[:, :head_width])
    q_blocks = sorted_query.reshape(group_count, GROUP, head_width)
    v_blocks = sorted_rows[:, head_width : 2 * head_width].reshape(group_count, GROUP, head_width)
    g_blocks = sorted_rows[:, 2 * head_width :].reshape(group_count, GROUP, head_width)
    prev_keys = jnp.concatenate([halo_keys[None], own_keys[:-1]], axis=0)
    prev_values = jnp.concatenate([halo_rows[None, :, head_width:], v_blocks[:-1]], axis=0)
    key_window = jnp.concatenate([own_keys, prev_keys], axis=1)
    value_window = jnp.concatenate([v_blocks, prev_values], axis=1)
    scores = (
        jnp.einsum("cqd,ckd->cqk", q_blocks, key_window, preferred_element_type=jnp.float32)
        * scale_factor
    )
    self_mask = jnp.arange(GROUP)[:, None] == jnp.arange(2 * GROUP)[None, :]
    scores = jnp.where(self_mask[None], masked_score, scores)
    probs = jax.nn.softmax(scores, axis=-1)
    dprob = jnp.einsum("cqd,ckd->cqk", g_blocks, value_window, preferred_element_type=jnp.float32)
    dscore = probs * (dprob - jnp.sum(probs * dprob, axis=-1, keepdims=True))
    probs_low = probs.astype(jnp.bfloat16)
    dscore_low = dscore.astype(jnp.bfloat16)
    dquery = (
        jnp.einsum("cqk,ckd->cqd", dscore_low, key_window, preferred_element_type=jnp.float32)
        * scale_factor
    )
    dkey_window = (
        jnp.einsum("cqk,cqd->ckd", dscore_low, q_blocks, preferred_element_type=jnp.float32)
        * scale_factor
    )
    dvalue_window = jnp.einsum(
        "cqk,cqd->ckd", probs_low, g_blocks, preferred_element_type=jnp.float32
    )
    grad_window = jnp.concatenate([dkey_window, dvalue_window], axis=-1)
    own_part = grad_window[:, :GROUP]
    later_part = grad_window[1:, GROUP:]
    outgoing = grad_window[0, GROUP:]
    incoming = shifted(outgoing, SEQ, -1)
    key_value = (own_part + jnp.concatenate([later_part, incoming[None]], axis=0)).reshape(
        tok_count, 2 * head_width
    )
    dquery_s = dquery.reshape(tok_count, head_width)
    dkey_s = key_value[:, :head_width]
    dvalue_s = key_value[:, head_width:]
    query_float = sorted_query.astype(jnp.float32)
    norm_s = jnp.sqrt(jnp.sum(query_float * query_float, axis=1, keepdims=True) + eps_norm)
    along = jnp.sum(query_float * dkey_s, axis=1, keepdims=True)
    dshared_s = dquery_s + dkey_s / norm_s - query_float * (along / norm_s**3)
    sorted_grads = jnp.concatenate(
        [dshared_s.astype(jnp.bfloat16), dvalue_s.astype(jnp.bfloat16)], axis=1
    )
    return_rows = sorted_grads[jnp.minimum(recv_slots, tok_count - 1)]
    back_rows = lax.all_to_all(return_rows, SEQ, split_axis=0, concat_axis=0, tiled=True)
    combined = back_rows[buffer_index]
    nz, ny, nc = (lax.axis_size(a) for a in SEQ)
    rows = feat_count // (nz * ny * nc)
    blocks = whole.reshape(tok_count, nz, ny, nc, rows)
    first = jnp.einsum(
        "pzyck,ph->cyzkh", blocks[..., : rows // 2], combined, preferred_element_type=jnp.float32
    )
    second = jnp.einsum(
        "pzyck,ph->czykh", blocks[..., rows // 2 :], combined, preferred_element_type=jnp.float32
    )
    partial = jnp.stack([first, second], axis=1)

    def reduce_over(value, axis):
        return jnp.sum(lax.all_to_all(value, axis, 0, 0, tiled=True), axis=0)

    halves = reduce_over(partial, "c")
    first = reduce_over(reduce_over(halves[0], "y"), "z")
    second = reduce_over(reduce_over(halves[1], "z"), "y")
    grads = jnp.concatenate([first, second], axis=0)
    return (grads[:, :head_width], grads[:, head_width:])


def split_mesh(mesh):
    devices = mesh.devices
    seq_n, head_n = devices.shape
    column = devices[:, 0]
    cores = sorted({d.core_on_chip for d in column})
    ys = sorted({d.coords[1] for d in column})
    nc, ny = len(cores), len(ys)
    nz = seq_n // (nc * ny)
    grid = devices.reshape(nz, ny, nc, head_n)
    for z in range(nz):
        for y in range(ny):
            for c in range(nc):
                d = grid[z, y, c, 0]
                assert d.core_on_chip == cores[c] and d.coords[1] == ys[y]
    return Mesh(grid, SEQ + ("head",))


def solution(mesh):
    fine = split_mesh(mesh)
    in_specs = (
        P(SEQ, "head"),
        P(None, "head"),
        P(None, "head"),
        P(SEQ, "head"),
        P("head", SEQ),
    )
    out_specs = (P(SEQ, "head"), P(SEQ, "head"))
    return jax.shard_map(
        per_device, mesh=fine, in_specs=in_specs, out_specs=out_specs, check_vma=False
    )
```

```python
import math

import jax
import jax.numpy as jnp
from jax import lax
from jax.sharding import Mesh
from jax.sharding import PartitionSpec as P

GROUP = 64

SEQ = ("z", "y", "c")


eps_norm = 1e-06
masked_score = -1000000000.0


def shifted(value, axis, steps):
    count = lax.axis_size(axis)
    pairs = [(source, (source + steps) % count) for source in range(count)]
    return lax.ppermute(value, axis, pairs)


def unit_keys(block):
    block_float = block.astype(jnp.float32)
    norm_rows = jnp.sqrt(jnp.sum(block_float * block_float, axis=1, keepdims=True) + eps_norm)
    return (block_float / norm_rows).astype(jnp.bfloat16)


def per_device(tokens, shared_weight, value_weight, head_grad, sorted_slot):
    tok_count = tokens.shape[0]
    head_n = lax.axis_size("head")
    spread = jnp.broadcast_to(tokens[None], (head_n,) + tokens.shape)
    gathered = lax.all_to_all(spread, "head", 0, 0, tiled=True)
    whole = gathered.transpose(1, 0, 2).reshape(tok_count, head_n * tokens.shape[1])
    feat_count = whole.shape[1]
    head_width = shared_weight.shape[1]
    peer_count = lax.axis_size(SEQ)
    capacity = 2 * tok_count // peer_count
    group_count = tok_count // GROUP
    tail_start = tok_count - GROUP
    scale_factor = 1.0 / math.sqrt(head_width)
    query = jnp.dot(whole, shared_weight, preferred_element_type=jnp.float32).astype(jnp.bfloat16)
    values = jnp.dot(whole, value_weight, preferred_element_type=jnp.float32).astype(jnp.bfloat16)
    slot_ids = sorted_slot[0]
    target = slot_ids // tok_count
    local_slot = slot_ids - target * tok_count
    peer_ids = jnp.arange(peer_count, dtype=jnp.int32)
    row_ids = jnp.arange(tok_count, dtype=jnp.int32)
    earlier_rows = (row_ids[:, None] > row_ids[None, :]).astype(jnp.bfloat16)
    every_row = jnp.ones((tok_count,), dtype=bool)
    one_hot = ((target[:, None] == peer_ids[None, :]) & every_row[:, None]).astype(jnp.bfloat16)
    before = jnp.dot(earlier_rows, one_hot, preferred_element_type=jnp.float32)
    buffer_index = target * capacity + jnp.sum(before * one_hot.astype(jnp.float32), axis=1).astype(
        jnp.int32
    )
    slot_block = jnp.zeros((tok_count, head_width), jnp.bfloat16).at[:, 0].set(
        local_slot.astype(jnp.bfloat16)
    )
    payload = jnp.concatenate([query, values, head_grad, slot_block], axis=1)
    buffer_ids = jnp.arange(peer_count * capacity, dtype=jnp.int32)
    to_buffer = (buffer_ids[:, None] == buffer_index[None, :]).astype(jnp.bfloat16)
    send_rows = jnp.dot(to_buffer, payload, preferred_element_type=jnp.float32).astype(jnp.bfloat16)
    empty = (buffer_ids[:, None] * 0 + jnp.arange(head_width)[None, :]) == 0
    used = jnp.sum(to_buffer.astype(jnp.float32), axis=1) > 0
    send_rows = send_rows.at[:, 3 * head_width :].set(
        jnp.where(
            empty & ~used[:, None],
            jnp.bfloat16(tok_count),
            send_rows[:, 3 * head_width :],
        )
    )
    recv_rows = lax.all_to_all(send_rows, SEQ, split_axis=0, concat_axis=0, tiled=True)
    recv_slots = recv_rows[:, 3 * head_width].astype(jnp.int32)
    to_sorted = (row_ids[:, None] == recv_slots[None, :]).astype(jnp.bfloat16)
    sorted_rows = jnp.dot(
        to_sorted, recv_rows[:, : 3 * head_width], preferred_element_type=jnp.float32
    ).astype(jnp.bfloat16)
    halo_rows = shifted(sorted_rows[tail_start:, : 2 * head_width], SEQ, 1)
    sorted_query = sorted_rows[:, :head_width]
    own_keys = unit_keys(sorted_query).reshape(group_count, GROUP, head_width)
    halo_keys = unit_keys(halo_rows[:, :head_width])
    q_blocks = sorted_query.reshape(group_count, GROUP, head_width)
    v_blocks = sorted_rows[:, head_width : 2 * head_width].reshape(group_count, GROUP, head_width)
    g_blocks = sorted_rows[:, 2 * head_width :].reshape(group_count, GROUP, head_width)
    prev_keys = jnp.concatenate([halo_keys[None], own_keys[:-1]], axis=0)
    prev_values = jnp.concatenate([halo_rows[None, :, head_width:], v_blocks[:-1]], axis=0)
    key_window = jnp.concatenate([own_keys, prev_keys], axis=1)
    value_window = jnp.concatenate([v_blocks, prev_values], axis=1)
    scores = (
        jnp.einsum("cqd,ckd->cqk", q_blocks, key_window, preferred_element_type=jnp.float32)
        * scale_factor
    )
    self_mask = jnp.arange(GROUP)[:, None] == jnp.arange(2 * GROUP)[None, :]
    scores = jnp.where(self_mask[None], masked_score, scores)
    probs = jax.nn.softmax(scores, axis=-1)
    dprob = jnp.einsum("cqd,ckd->cqk", g_blocks, value_window, preferred_element_type=jnp.float32)
    dscore = probs * (dprob - jnp.sum(probs * dprob, axis=-1, keepdims=True))
    probs_low = probs.astype(jnp.bfloat16)
    dscore_low = dscore.astype(jnp.bfloat16)
    dquery = (
        jnp.einsum("cqk,ckd->cqd", dscore_low, key_window, preferred_element_type=jnp.float32)
        * scale_factor
    )
    dkey_window = (
        jnp.einsum("cqk,cqd->ckd", dscore_low, q_blocks, preferred_element_type=jnp.float32)
        * scale_factor
    )
    dvalue_window = jnp.einsum(
        "cqk,cqd->ckd", probs_low, g_blocks, preferred_element_type=jnp.float32
    )
    grad_window = jnp.concatenate([dkey_window, dvalue_window], axis=-1)
    own_part = grad_window[:, :GROUP]
    later_part = grad_window[1:, GROUP:]
    outgoing = grad_window[0, GROUP:]
    incoming = shifted(outgoing, SEQ, -1)
    key_value = (own_part + jnp.concatenate([later_part, incoming[None]], axis=0)).reshape(
        tok_count, 2 * head_width
    )
    dquery_s = dquery.reshape(tok_count, head_width)
    dkey_s = key_value[:, :head_width]
    dvalue_s = key_value[:, head_width:]
    query_float = sorted_query.astype(jnp.float32)
    norm_s = jnp.sqrt(jnp.sum(query_float * query_float, axis=1, keepdims=True) + eps_norm)
    along = jnp.sum(query_float * dkey_s, axis=1, keepdims=True)
    dshared_s = dquery_s + dkey_s / norm_s - query_float * (along / norm_s**3)
    sorted_grads = jnp.concatenate(
        [dshared_s.astype(jnp.bfloat16), dvalue_s.astype(jnp.bfloat16)], axis=1
    )
    return_rows = lax.dot_general(
        to_sorted, sorted_grads, (((0,), (0,)), ((), ())), preferred_element_type=jnp.float32
    ).astype(jnp.bfloat16)
    back_rows = lax.all_to_all(return_rows, SEQ, split_axis=0, concat_axis=0, tiled=True)
    combined = lax.dot_general(
        to_buffer, back_rows, (((0,), (0,)), ((), ())), preferred_element_type=jnp.float32
    ).astype(jnp.bfloat16)
    nz, ny, nc = (lax.axis_size(a) for a in SEQ)
    rows = feat_count // (nz * ny * nc)
    blocks = whole.reshape(tok_count, nz, ny, nc, rows)
    grads = jnp.einsum("pzyck,ph->cyzkh", blocks, combined, preferred_element_type=jnp.float32)
    for axis in ("c", "y", "z"):
        grads = jnp.sum(lax.all_to_all(grads, axis, 0, 0, tiled=True), axis=0)
    grads = grads.reshape(rows, 2 * head_width)
    return (grads[:, :head_width], grads[:, head_width:])


def split_mesh(mesh):
    devices = mesh.devices
    seq_n, head_n = devices.shape
    column = devices[:, 0]
    cores = sorted({d.core_on_chip for d in column})
    ys = sorted({d.coords[1] for d in column})
    nc, ny = len(cores), len(ys)
    nz = seq_n // (nc * ny)
    grid = devices.reshape(nz, ny, nc, head_n)
    for z in range(nz):
        for y in range(ny):
            for c in range(nc):
                d = grid[z, y, c, 0]
                assert d.core_on_chip == cores[c] and d.coords[1] == ys[y]
    return Mesh(grid, SEQ + ("head",))


def solution(mesh):
    fine = split_mesh(mesh)
    in_specs = (
        P(SEQ, "head"),
        P(None, "head"),
        P(None, "head"),
        P(SEQ, "head"),
        P("head", SEQ),
    )
    out_specs = (P(SEQ, "head"), P(SEQ, "head"))
    return jax.shard_map(
        per_device, mesh=fine, in_specs=in_specs, out_specs=out_specs, check_vma=False
    )
```

```python
import math

import jax
import jax.numpy as jnp
from jax import lax
from jax.sharding import Mesh
from jax.sharding import PartitionSpec as P

GROUP = 64

SEQ = ("z", "y", "c")


eps_norm = 1e-06
masked_score = -1000000000.0


def shifted(value, axis, steps):
    count = lax.axis_size(axis)
    pairs = [(source, (source + steps) % count) for source in range(count)]
    return lax.ppermute(value, axis, pairs)


def unit_keys(block):
    block_float = block.astype(jnp.float32)
    norm_rows = jnp.sqrt(jnp.sum(block_float * block_float, axis=1, keepdims=True) + eps_norm)
    return (block_float / norm_rows).astype(jnp.bfloat16)


def per_device(tokens, shared_weight, value_weight, head_grad, sorted_slot):
    tok_count = tokens.shape[0]
    head_n = lax.axis_size("head")
    spread = jnp.broadcast_to(tokens[None], (head_n,) + tokens.shape)
    gathered = lax.all_to_all(spread, "head", 0, 0, tiled=True)
    whole = gathered.transpose(1, 0, 2).reshape(tok_count, head_n * tokens.shape[1])
    feat_count = whole.shape[1]
    head_width = shared_weight.shape[1]
    peer_count = lax.axis_size(SEQ)
    capacity = 2 * tok_count // peer_count
    group_count = tok_count // GROUP
    tail_start = tok_count - GROUP
    scale_factor = 1.0 / math.sqrt(head_width)
    query = jnp.dot(whole, shared_weight, preferred_element_type=jnp.float32).astype(jnp.bfloat16)
    values = jnp.dot(whole, value_weight, preferred_element_type=jnp.float32).astype(jnp.bfloat16)
    slot_ids = sorted_slot[0]
    target = slot_ids // tok_count
    local_slot = slot_ids - target * tok_count
    peer_ids = jnp.arange(peer_count, dtype=jnp.int32)
    row_ids = jnp.arange(tok_count, dtype=jnp.int32)
    earlier_rows = (row_ids[:, None] > row_ids[None, :]).astype(jnp.bfloat16)
    every_row = jnp.ones((tok_count,), dtype=bool)
    one_hot = ((target[:, None] == peer_ids[None, :]) & every_row[:, None]).astype(jnp.bfloat16)
    before = jnp.dot(earlier_rows, one_hot, preferred_element_type=jnp.float32)
    buffer_index = target * capacity + jnp.sum(before * one_hot.astype(jnp.float32), axis=1).astype(
        jnp.int32
    )
    slot_block = jnp.zeros((tok_count, head_width), jnp.bfloat16).at[:, 0].set(
        local_slot.astype(jnp.bfloat16)
    )
    payload = jnp.concatenate([query, values, head_grad, slot_block], axis=1)
    buffer_ids = jnp.arange(peer_count * capacity, dtype=jnp.int32)
    to_buffer = (buffer_ids[:, None] == buffer_index[None, :]).astype(jnp.bfloat16)
    send_rows = jnp.dot(to_buffer, payload, preferred_element_type=jnp.float32).astype(jnp.bfloat16)
    empty = (buffer_ids[:, None] * 0 + jnp.arange(head_width)[None, :]) == 0
    used = jnp.sum(to_buffer.astype(jnp.float32), axis=1) > 0
    send_rows = send_rows.at[:, 3 * head_width :].set(
        jnp.where(
            empty & ~used[:, None],
            jnp.bfloat16(tok_count),
            send_rows[:, 3 * head_width :],
        )
    )
    recv_rows = lax.all_to_all(send_rows, SEQ, split_axis=0, concat_axis=0, tiled=True)
    recv_slots = recv_rows[:, 3 * head_width].astype(jnp.int32)
    to_sorted = (row_ids[:, None] == recv_slots[None, :]).astype(jnp.bfloat16)
    sorted_rows = jnp.dot(
        to_sorted, recv_rows[:, : 3 * head_width], preferred_element_type=jnp.float32
    ).astype(jnp.bfloat16)
    halo_rows = shifted(sorted_rows[tail_start:, : 2 * head_width], SEQ, 1)
    sorted_query = sorted_rows[:, :head_width]
    own_keys = unit_keys(sorted_query).reshape(group_count, GROUP, head_width)
    halo_keys = unit_keys(halo_rows[:, :head_width])
    q_blocks = sorted_query.reshape(group_count, GROUP, head_width)
    v_blocks = sorted_rows[:, head_width : 2 * head_width].reshape(group_count, GROUP, head_width)
    g_blocks = sorted_rows[:, 2 * head_width :].reshape(group_count, GROUP, head_width)
    prev_keys = jnp.concatenate([halo_keys[None], own_keys[:-1]], axis=0)
    prev_values = jnp.concatenate([halo_rows[None, :, head_width:], v_blocks[:-1]], axis=0)
    key_window = jnp.concatenate([own_keys, prev_keys], axis=1)
    value_window = jnp.concatenate([v_blocks, prev_values], axis=1)
    scores = (
        jnp.einsum("cqd,ckd->cqk", q_blocks, key_window, preferred_element_type=jnp.float32)
        * scale_factor
    )
    self_mask = jnp.arange(GROUP)[:, None] == jnp.arange(2 * GROUP)[None, :]
    scores = jnp.where(self_mask[None], masked_score, scores)
    probs = jax.nn.softmax(scores, axis=-1)
    dprob = jnp.einsum("cqd,ckd->cqk", g_blocks, value_window, preferred_element_type=jnp.float32)
    dscore = probs * (dprob - jnp.sum(probs * dprob, axis=-1, keepdims=True))
    probs_low = probs.astype(jnp.bfloat16)
    dscore_low = dscore.astype(jnp.bfloat16)
    dquery = (
        jnp.einsum("cqk,ckd->cqd", dscore_low, key_window, preferred_element_type=jnp.float32)
        * scale_factor
    )
    dkey_window = (
        jnp.einsum("cqk,cqd->ckd", dscore_low, q_blocks, preferred_element_type=jnp.float32)
        * scale_factor
    )
    dvalue_window = jnp.einsum(
        "cqk,cqd->ckd", probs_low, g_blocks, preferred_element_type=jnp.float32
    )
    grad_window = jnp.concatenate([dkey_window, dvalue_window], axis=-1)
    own_part = grad_window[:, :GROUP]
    later_part = grad_window[1:, GROUP:]
    outgoing = grad_window[0, GROUP:]
    incoming = shifted(outgoing, SEQ, -1)
    key_value = (own_part + jnp.concatenate([later_part, incoming[None]], axis=0)).reshape(
        tok_count, 2 * head_width
    )
    dquery_s = dquery.reshape(tok_count, head_width)
    dkey_s = key_value[:, :head_width]
    dvalue_s = key_value[:, head_width:]
    query_float = sorted_query.astype(jnp.float32)
    norm_s = jnp.sqrt(jnp.sum(query_float * query_float, axis=1, keepdims=True) + eps_norm)
    along = jnp.sum(query_float * dkey_s, axis=1, keepdims=True)
    dshared_s = dquery_s + dkey_s / norm_s - query_float * (along / norm_s**3)
    sorted_grads = jnp.concatenate(
        [dshared_s.astype(jnp.bfloat16), dvalue_s.astype(jnp.bfloat16)], axis=1
    )
    return_rows = lax.dot_general(
        to_sorted, sorted_grads, (((0,), (0,)), ((), ())), preferred_element_type=jnp.float32
    ).astype(jnp.bfloat16)
    back_rows = lax.all_to_all(return_rows, SEQ, split_axis=0, concat_axis=0, tiled=True)
    combined = lax.dot_general(
        to_buffer, back_rows, (((0,), (0,)), ((), ())), preferred_element_type=jnp.float32
    ).astype(jnp.bfloat16)
    nz, ny, nc = (lax.axis_size(a) for a in SEQ)
    rows = feat_count // (nz * ny * nc)
    blocks = whole.reshape(tok_count, nz, ny, nc, rows)
    grads = jnp.einsum("pzyck,ph->cyzkh", blocks, combined, preferred_element_type=jnp.float32)
    grads = jnp.sum(lax.all_to_all(grads, "c", 0, 0, tiled=True), axis=0)
    grads = jnp.sum(
        lax.all_to_all(grads.astype(jnp.bfloat16), "y", 0, 0, tiled=True).astype(jnp.float32), axis=0
    )
    grads = jnp.sum(lax.all_to_all(grads, "z", 0, 0, tiled=True), axis=0)
    grads = grads.reshape(rows, 2 * head_width)
    return (grads[:, :head_width], grads[:, head_width:])


def split_mesh(mesh):
    devices = mesh.devices
    seq_n, head_n = devices.shape
    column = devices[:, 0]
    cores = sorted({d.core_on_chip for d in column})
    ys = sorted({d.coords[1] for d in column})
    nc, ny = len(cores), len(ys)
    nz = seq_n // (nc * ny)
    grid = devices.reshape(nz, ny, nc, head_n)
    for z in range(nz):
        for y in range(ny):
            for c in range(nc):
                d = grid[z, y, c, 0]
                assert d.core_on_chip == cores[c] and d.coords[1] == ys[y]
    return Mesh(grid, SEQ + ("head",))


def solution(mesh):
    fine = split_mesh(mesh)
    in_specs = (
        P(SEQ, "head"),
        P(None, "head"),
        P(None, "head"),
        P(SEQ, "head"),
        P("head", SEQ),
    )
    out_specs = (P(SEQ, "head"), P(SEQ, "head"))
    return jax.shard_map(
        per_device, mesh=fine, in_specs=in_specs, out_specs=out_specs, check_vma=False
    )
```

```python
import math

import jax
import jax.numpy as jnp
from jax import lax
from jax.sharding import Mesh
from jax.sharding import PartitionSpec as P

GROUP = 64

SEQ = ("z", "y", "c")


eps_norm = 1e-06
masked_score = -1000000000.0


def shifted(value, axis, steps):
    count = lax.axis_size(axis)
    pairs = [(source, (source + steps) % count) for source in range(count)]
    return lax.ppermute(value, axis, pairs)


def unit_keys(block):
    block_float = block.astype(jnp.float32)
    norm_rows = jnp.sqrt(jnp.sum(block_float * block_float, axis=1, keepdims=True) + eps_norm)
    return (block_float / norm_rows).astype(jnp.bfloat16)


def per_device(tokens, shared_weight, value_weight, head_grad, sorted_slot):
    tok_count = tokens.shape[0]
    head_n = lax.axis_size("head")
    spread = jnp.broadcast_to(tokens[None], (head_n,) + tokens.shape)
    gathered = lax.all_to_all(spread, "head", 0, 0, tiled=True)
    whole = gathered.transpose(1, 0, 2).reshape(tok_count, head_n * tokens.shape[1])
    feat_count = whole.shape[1]
    head_width = shared_weight.shape[1]
    peer_count = lax.axis_size(SEQ)
    capacity = 2 * tok_count // peer_count
    group_count = tok_count // GROUP
    tail_start = tok_count - GROUP
    scale_factor = 1.0 / math.sqrt(head_width)
    query = jnp.dot(whole, shared_weight, preferred_element_type=jnp.float32).astype(jnp.bfloat16)
    values = jnp.dot(whole, value_weight, preferred_element_type=jnp.float32).astype(jnp.bfloat16)
    slot_ids = sorted_slot[0]
    target = slot_ids // tok_count
    local_slot = slot_ids - target * tok_count
    peer_ids = jnp.arange(peer_count, dtype=jnp.int32)
    row_ids = jnp.arange(tok_count, dtype=jnp.int32)
    earlier_rows = (row_ids[:, None] > row_ids[None, :]).astype(jnp.bfloat16)
    every_row = jnp.ones((tok_count,), dtype=bool)
    one_hot = ((target[:, None] == peer_ids[None, :]) & every_row[:, None]).astype(jnp.bfloat16)
    before = jnp.dot(earlier_rows, one_hot, preferred_element_type=jnp.float32)
    buffer_index = target * capacity + jnp.sum(before * one_hot.astype(jnp.float32), axis=1).astype(
        jnp.int32
    )
    slot_block = jnp.zeros((tok_count, head_width), jnp.bfloat16).at[:, 0].set(
        local_slot.astype(jnp.bfloat16)
    )
    payload = jnp.concatenate([query, values, head_grad, slot_block], axis=1)
    buffer_ids = jnp.arange(peer_count * capacity, dtype=jnp.int32)
    to_buffer = (buffer_ids[:, None] == buffer_index[None, :]).astype(jnp.bfloat16)
    send_rows = jnp.dot(to_buffer, payload, preferred_element_type=jnp.float32).astype(jnp.bfloat16)
    empty = (buffer_ids[:, None] * 0 + jnp.arange(head_width)[None, :]) == 0
    used = jnp.sum(to_buffer.astype(jnp.float32), axis=1) > 0
    send_rows = send_rows.at[:, 3 * head_width :].set(
        jnp.where(
            empty & ~used[:, None],
            jnp.bfloat16(tok_count),
            send_rows[:, 3 * head_width :],
        )
    )
    recv_rows = lax.all_to_all(send_rows, SEQ, split_axis=0, concat_axis=0, tiled=True)
    recv_slots = recv_rows[:, 3 * head_width].astype(jnp.int32)
    to_sorted = (row_ids[:, None] == recv_slots[None, :]).astype(jnp.bfloat16)
    sorted_rows = jnp.dot(
        to_sorted, recv_rows[:, : 3 * head_width], preferred_element_type=jnp.float32
    ).astype(jnp.bfloat16)
    halo_rows = shifted(sorted_rows[tail_start:, : 2 * head_width], SEQ, 1)
    sorted_query = sorted_rows[:, :head_width]
    own_keys = unit_keys(sorted_query).reshape(group_count, GROUP, head_width)
    halo_keys = unit_keys(halo_rows[:, :head_width])
    q_blocks = sorted_query.reshape(group_count, GROUP, head_width)
    v_blocks = sorted_rows[:, head_width : 2 * head_width].reshape(group_count, GROUP, head_width)
    g_blocks = sorted_rows[:, 2 * head_width :].reshape(group_count, GROUP, head_width)
    prev_keys = jnp.concatenate([halo_keys[None], own_keys[:-1]], axis=0)
    prev_values = jnp.concatenate([halo_rows[None, :, head_width:], v_blocks[:-1]], axis=0)
    key_window = jnp.concatenate([own_keys, prev_keys], axis=1)
    value_window = jnp.concatenate([v_blocks, prev_values], axis=1)
    scores = (
        jnp.einsum("cqd,ckd->cqk", q_blocks, key_window, preferred_element_type=jnp.float32)
        * scale_factor
    )
    self_mask = jnp.arange(GROUP)[:, None] == jnp.arange(2 * GROUP)[None, :]
    scores = jnp.where(self_mask[None], masked_score, scores)
    probs = jax.nn.softmax(scores, axis=-1)
    dprob = jnp.einsum("cqd,ckd->cqk", g_blocks, value_window, preferred_element_type=jnp.float32)
    dscore = probs * (dprob - jnp.sum(probs * dprob, axis=-1, keepdims=True))
    probs_low = probs.astype(jnp.bfloat16)
    dscore_low = dscore.astype(jnp.bfloat16)
    dquery = (
        jnp.einsum("cqk,ckd->cqd", dscore_low, key_window, preferred_element_type=jnp.float32)
        * scale_factor
    )
    dkey_window = (
        jnp.einsum("cqk,cqd->ckd", dscore_low, q_blocks, preferred_element_type=jnp.float32)
        * scale_factor
    )
    dvalue_window = jnp.einsum(
        "cqk,cqd->ckd", probs_low, g_blocks, preferred_element_type=jnp.float32
    )
    grad_window = jnp.concatenate([dkey_window, dvalue_window], axis=-1)
    own_part = grad_window[:, :GROUP]
    later_part = grad_window[1:, GROUP:]
    outgoing = grad_window[0, GROUP:]
    incoming = shifted(outgoing, SEQ, -1)
    key_value = (own_part + jnp.concatenate([later_part, incoming[None]], axis=0)).reshape(
        tok_count, 2 * head_width
    )
    dquery_s = dquery.reshape(tok_count, head_width)
    dkey_s = key_value[:, :head_width]
    dvalue_s = key_value[:, head_width:]
    query_float = sorted_query.astype(jnp.float32)
    norm_s = jnp.sqrt(jnp.sum(query_float * query_float, axis=1, keepdims=True) + eps_norm)
    along = jnp.sum(query_float * dkey_s, axis=1, keepdims=True)
    dshared_s = dquery_s + dkey_s / norm_s - query_float * (along / norm_s**3)
    sorted_grads = jnp.concatenate(
        [dshared_s.astype(jnp.bfloat16), dvalue_s.astype(jnp.bfloat16)], axis=1
    )
    return_rows = lax.dot_general(
        to_sorted, sorted_grads, (((0,), (0,)), ((), ())), preferred_element_type=jnp.float32
    ).astype(jnp.bfloat16)
    nz, ny, nc = (lax.axis_size(a) for a in SEQ)
    my_core = lax.axis_index("c")
    by_peer = return_rows.reshape(peer_count, capacity, 2 * head_width)
    peer_core = jnp.arange(peer_count) % nc
    peer_chip = jnp.arange(peer_count) - peer_core
    shifted_peers = [peer_chip + (peer_core + j) % nc for j in range(nc)]
    to_chip = jnp.stack([by_peer[p] for p in shifted_peers], axis=1)
    back_rows = lax.all_to_all(to_chip, SEQ, split_axis=0, concat_axis=0, tiled=True)
    rows = feat_count // (nz * ny * nc)
    blocks = whole.reshape(tok_count, nz, ny, nc, rows).transpose(3, 0, 2, 1, 4)
    shares = blocks.reshape(nc, tok_count, ny * nz * rows)
    index_block = jnp.zeros((tok_count, head_width), jnp.bfloat16).at[:, 0].set(
        buffer_index.astype(jnp.bfloat16)
    )
    outgoing_shares = jnp.concatenate(
        [shares, jnp.broadcast_to(index_block[None], (nc, tok_count, head_width))], axis=2
    )
    chip_shares = lax.all_to_all(outgoing_shares, "c", 0, 0, tiled=True)
    grads = jnp.zeros((ny * nz * rows, 2 * head_width), jnp.float32)
    for source in range(nc):
        offset = (source - my_core) % nc
        rows_in = jnp.take(back_rows, offset, axis=1).reshape(peer_count * capacity, 2 * head_width)
        source_index = chip_shares[source, :, ny * nz * rows].astype(jnp.int32)
        source_buffer = (buffer_ids[:, None] == source_index[None, :]).astype(jnp.bfloat16)
        source_grads = lax.dot_general(
            source_buffer, rows_in, (((0,), (0,)), ((), ())), preferred_element_type=jnp.float32
        ).astype(jnp.bfloat16)
        grads = grads + lax.dot_general(
            chip_shares[source, :, : ny * nz * rows],
            source_grads,
            (((0,), (0,)), ((), ())),
            preferred_element_type=jnp.float32,
        )
    grads = grads.reshape(ny, nz, rows, 2 * head_width)
    grads = jnp.sum(
        lax.all_to_all(grads.astype(jnp.bfloat16), "y", 0, 0, tiled=True).astype(jnp.float32), axis=0
    )
    grads = jnp.sum(lax.all_to_all(grads, "z", 0, 0, tiled=True), axis=0)
    grads = grads.reshape(rows, 2 * head_width)
    return (grads[:, :head_width], grads[:, head_width:])


def split_mesh(mesh):
    devices = mesh.devices
    seq_n, head_n = devices.shape
    column = devices[:, 0]
    cores = sorted({d.core_on_chip for d in column})
    ys = sorted({d.coords[1] for d in column})
    nc, ny = len(cores), len(ys)
    nz = seq_n // (nc * ny)
    grid = devices.reshape(nz, ny, nc, head_n)
    for z in range(nz):
        for y in range(ny):
            for c in range(nc):
                d = grid[z, y, c, 0]
                assert d.core_on_chip == cores[c] and d.coords[1] == ys[y]
    return Mesh(grid, SEQ + ("head",))


def solution(mesh):
    fine = split_mesh(mesh)
    in_specs = (
        P(SEQ, "head"),
        P(None, "head"),
        P(None, "head"),
        P(SEQ, "head"),
        P("head", SEQ),
    )
    out_specs = (P(SEQ, "head"), P(SEQ, "head"))
    return jax.shard_map(
        per_device, mesh=fine, in_specs=in_specs, out_specs=out_specs, check_vma=False
    )
```

```python
import math

import jax
import jax.numpy as jnp
from jax import lax
from jax.sharding import Mesh
from jax.sharding import PartitionSpec as P

GROUP = 64

SEQ = ("z", "y", "c")


eps_norm = 1e-06
masked_score = -1000000000.0


def shifted(value, axis, steps):
    count = lax.axis_size(axis)
    pairs = [(source, (source + steps) % count) for source in range(count)]
    return lax.ppermute(value, axis, pairs)


def unit_keys(block):
    block_float = block.astype(jnp.float32)
    norm_rows = jnp.sqrt(jnp.sum(block_float * block_float, axis=1, keepdims=True) + eps_norm)
    return (block_float / norm_rows).astype(jnp.bfloat16)


def per_device(tokens, shared_weight, value_weight, head_grad, sorted_slot):
    tok_count = tokens.shape[0]
    head_n = lax.axis_size("head")
    spread = jnp.broadcast_to(tokens[None], (head_n,) + tokens.shape)
    gathered = lax.all_to_all(spread, "head", 0, 0, tiled=True)
    whole = gathered.transpose(1, 0, 2).reshape(tok_count, head_n * tokens.shape[1])
    feat_count = whole.shape[1]
    head_width = shared_weight.shape[1]
    peer_count = lax.axis_size(SEQ)
    capacity = 2 * tok_count // peer_count
    group_count = tok_count // GROUP
    tail_start = tok_count - GROUP
    scale_factor = 1.0 / math.sqrt(head_width)
    query = jnp.dot(whole, shared_weight, preferred_element_type=jnp.float32).astype(jnp.bfloat16)
    values = jnp.dot(whole, value_weight, preferred_element_type=jnp.float32).astype(jnp.bfloat16)
    slot_ids = sorted_slot[0]
    target = slot_ids // tok_count
    local_slot = slot_ids - target * tok_count
    peer_ids = jnp.arange(peer_count, dtype=jnp.int32)
    row_ids = jnp.arange(tok_count, dtype=jnp.int32)
    earlier_rows = (row_ids[:, None] > row_ids[None, :]).astype(jnp.bfloat16)
    every_row = jnp.ones((tok_count,), dtype=bool)
    one_hot = ((target[:, None] == peer_ids[None, :]) & every_row[:, None]).astype(jnp.bfloat16)
    before = jnp.dot(earlier_rows, one_hot, preferred_element_type=jnp.float32)
    buffer_index = target * capacity + jnp.sum(before * one_hot.astype(jnp.float32), axis=1).astype(
        jnp.int32
    )
    slot_block = jnp.zeros((tok_count, head_width), jnp.bfloat16).at[:, 0].set(
        local_slot.astype(jnp.bfloat16)
    )
    payload = jnp.concatenate([query, values, head_grad, slot_block], axis=1)
    buffer_ids = jnp.arange(peer_count * capacity, dtype=jnp.int32)
    to_buffer = (buffer_ids[:, None] == buffer_index[None, :]).astype(jnp.bfloat16)
    send_rows = jnp.dot(to_buffer, payload, preferred_element_type=jnp.float32).astype(jnp.bfloat16)
    empty = (buffer_ids[:, None] * 0 + jnp.arange(head_width)[None, :]) == 0
    used = jnp.sum(to_buffer.astype(jnp.float32), axis=1) > 0
    send_rows = send_rows.at[:, 3 * head_width :].set(
        jnp.where(
            empty & ~used[:, None],
            jnp.bfloat16(tok_count),
            send_rows[:, 3 * head_width :],
        )
    )
    recv_rows = lax.all_to_all(send_rows, SEQ, split_axis=0, concat_axis=0, tiled=True)
    recv_slots = recv_rows[:, 3 * head_width].astype(jnp.int32)
    to_sorted = (row_ids[:, None] == recv_slots[None, :]).astype(jnp.bfloat16)
    sorted_rows = jnp.dot(
        to_sorted, recv_rows[:, : 3 * head_width], preferred_element_type=jnp.float32
    ).astype(jnp.bfloat16)
    halo_rows = shifted(sorted_rows[tail_start:, : 2 * head_width], SEQ, 1)
    sorted_query = sorted_rows[:, :head_width]
    own_keys = unit_keys(sorted_query).reshape(group_count, GROUP, head_width)
    halo_keys = unit_keys(halo_rows[:, :head_width])
    q_blocks = sorted_query.reshape(group_count, GROUP, head_width)
    v_blocks = sorted_rows[:, head_width : 2 * head_width].reshape(group_count, GROUP, head_width)
    g_blocks = sorted_rows[:, 2 * head_width :].reshape(group_count, GROUP, head_width)
    prev_keys = jnp.concatenate([halo_keys[None], own_keys[:-1]], axis=0)
    prev_values = jnp.concatenate([halo_rows[None, :, head_width:], v_blocks[:-1]], axis=0)
    key_window = jnp.concatenate([own_keys, prev_keys], axis=1)
    value_window = jnp.concatenate([v_blocks, prev_values], axis=1)
    scores = (
        jnp.einsum("cqd,ckd->cqk", q_blocks, key_window, preferred_element_type=jnp.float32)
        * scale_factor
    )
    self_mask = jnp.arange(GROUP)[:, None] == jnp.arange(2 * GROUP)[None, :]
    scores = jnp.where(self_mask[None], masked_score, scores)
    probs = jax.nn.softmax(scores, axis=-1)
    dprob = jnp.einsum("cqd,ckd->cqk", g_blocks, value_window, preferred_element_type=jnp.float32)
    dscore = probs * (dprob - jnp.sum(probs * dprob, axis=-1, keepdims=True))
    probs_low = probs.astype(jnp.bfloat16)
    dscore_low = dscore.astype(jnp.bfloat16)
    dquery = (
        jnp.einsum("cqk,ckd->cqd", dscore_low, key_window, preferred_element_type=jnp.float32)
        * scale_factor
    )
    dkey_window = (
        jnp.einsum("cqk,cqd->ckd", dscore_low, q_blocks, preferred_element_type=jnp.float32)
        * scale_factor
    )
    dvalue_window = jnp.einsum(
        "cqk,cqd->ckd", probs_low, g_blocks, preferred_element_type=jnp.float32
    )
    grad_window = jnp.concatenate([dkey_window, dvalue_window], axis=-1)
    own_part = grad_window[:, :GROUP]
    later_part = grad_window[1:, GROUP:]
    outgoing = grad_window[0, GROUP:]
    incoming = shifted(outgoing, SEQ, -1)
    key_value = (own_part + jnp.concatenate([later_part, incoming[None]], axis=0)).reshape(
        tok_count, 2 * head_width
    )
    dquery_s = dquery.reshape(tok_count, head_width)
    dkey_s = key_value[:, :head_width]
    dvalue_s = key_value[:, head_width:]
    query_float = sorted_query.astype(jnp.float32)
    norm_s = jnp.sqrt(jnp.sum(query_float * query_float, axis=1, keepdims=True) + eps_norm)
    along = jnp.sum(query_float * dkey_s, axis=1, keepdims=True)
    dshared_s = dquery_s + dkey_s / norm_s - query_float * (along / norm_s**3)
    sorted_grads = jnp.concatenate(
        [dshared_s.astype(jnp.bfloat16), dvalue_s.astype(jnp.bfloat16)], axis=1
    )
    return_rows = lax.dot_general(
        to_sorted, sorted_grads, (((0,), (0,)), ((), ())), preferred_element_type=jnp.float32
    ).astype(jnp.bfloat16)
    nz, ny, nc = (lax.axis_size(a) for a in SEQ)
    my_core = lax.axis_index("c")
    by_peer = return_rows.reshape(peer_count, capacity, 2 * head_width)
    peer_core = jnp.arange(peer_count) % nc
    peer_chip = jnp.arange(peer_count) - peer_core
    shifted_peers = [peer_chip + (peer_core + j) % nc for j in range(nc)]
    to_chip = jnp.stack([by_peer[p] for p in shifted_peers], axis=1)
    back_rows = lax.all_to_all(to_chip, SEQ, split_axis=0, concat_axis=0, tiled=True)
    rows = feat_count // (nz * ny * nc)
    blocks = whole.reshape(tok_count, nz, ny, nc, rows).transpose(3, 0, 1, 2, 4)
    shares = blocks.reshape(nc, tok_count, ny * nz * rows)
    index_block = jnp.zeros((tok_count, head_width), jnp.bfloat16).at[:, 0].set(
        buffer_index.astype(jnp.bfloat16)
    )
    outgoing_shares = jnp.concatenate(
        [shares, jnp.broadcast_to(index_block[None], (nc, tok_count, head_width))], axis=2
    )
    chip_shares = lax.all_to_all(outgoing_shares, "c", 0, 0, tiled=True)
    grads = jnp.zeros((ny * nz * rows, 2 * head_width), jnp.float32)
    for source in range(nc):
        offset = (source - my_core) % nc
        rows_in = jnp.take(back_rows, offset, axis=1).reshape(peer_count * capacity, 2 * head_width)
        source_index = chip_shares[source, :, ny * nz * rows].astype(jnp.int32)
        source_buffer = (buffer_ids[:, None] == source_index[None, :]).astype(jnp.bfloat16)
        source_grads = lax.dot_general(
            source_buffer, rows_in, (((0,), (0,)), ((), ())), preferred_element_type=jnp.float32
        ).astype(jnp.bfloat16)
        grads = grads + lax.dot_general(
            chip_shares[source, :, : ny * nz * rows],
            source_grads,
            (((0,), (0,)), ((), ())),
            preferred_element_type=jnp.float32,
        )
    grads = grads.reshape(nz * ny, rows, 2 * head_width)
    grads = jnp.sum(
        lax.all_to_all(grads.astype(jnp.bfloat16), ("z", "y"), 0, 0, tiled=True).astype(jnp.float32),
        axis=0,
    )
    grads = grads.reshape(rows, 2 * head_width)
    return (grads[:, :head_width], grads[:, head_width:])


def split_mesh(mesh):
    devices = mesh.devices
    seq_n, head_n = devices.shape
    column = devices[:, 0]
    cores = sorted({d.core_on_chip for d in column})
    ys = sorted({d.coords[1] for d in column})
    nc, ny = len(cores), len(ys)
    nz = seq_n // (nc * ny)
    grid = devices.reshape(nz, ny, nc, head_n)
    for z in range(nz):
        for y in range(ny):
            for c in range(nc):
                d = grid[z, y, c, 0]
                assert d.core_on_chip == cores[c] and d.coords[1] == ys[y]
    return Mesh(grid, SEQ + ("head",))


def solution(mesh):
    fine = split_mesh(mesh)
    in_specs = (
        P(SEQ, "head"),
        P(None, "head"),
        P(None, "head"),
        P(SEQ, "head"),
        P("head", SEQ),
    )
    out_specs = (P(SEQ, "head"), P(SEQ, "head"))
    return jax.shard_map(
        per_device, mesh=fine, in_specs=in_specs, out_specs=out_specs, check_vma=False
    )
```

```python
import math

import jax
import jax.numpy as jnp
from jax import lax
from jax.sharding import Mesh
from jax.sharding import PartitionSpec as P

GROUP = 64

SEQ = ("z", "y", "c")


eps_norm = 1e-06
masked_score = -1000000000.0


def shifted(value, axis, steps):
    count = lax.axis_size(axis)
    pairs = [(source, (source + steps) % count) for source in range(count)]
    return lax.ppermute(value, axis, pairs)


def unit_keys(block):
    block_float = block.astype(jnp.float32)
    norm_rows = jnp.sqrt(jnp.sum(block_float * block_float, axis=1, keepdims=True) + eps_norm)
    return (block_float / norm_rows).astype(jnp.bfloat16)


def per_device(tokens, shared_weight, value_weight, head_grad, sorted_slot):
    tok_count = tokens.shape[0]
    head_n = lax.axis_size("head")
    spread = jnp.broadcast_to(tokens[None], (head_n,) + tokens.shape)
    gathered = lax.all_to_all(spread, "head", 0, 0, tiled=True)
    whole = gathered.transpose(1, 0, 2).reshape(tok_count, head_n * tokens.shape[1])
    feat_count = whole.shape[1]
    head_width = shared_weight.shape[1]
    peer_count = lax.axis_size(SEQ)
    capacity = 2 * tok_count // peer_count
    group_count = tok_count // GROUP
    tail_start = tok_count - GROUP
    scale_factor = 1.0 / math.sqrt(head_width)
    query = jnp.dot(whole, shared_weight, preferred_element_type=jnp.float32).astype(jnp.bfloat16)
    values = jnp.dot(whole, value_weight, preferred_element_type=jnp.float32).astype(jnp.bfloat16)
    slot_ids = sorted_slot[0]
    target = slot_ids // tok_count
    local_slot = slot_ids - target * tok_count
    peer_ids = jnp.arange(peer_count, dtype=jnp.int32)
    row_ids = jnp.arange(tok_count, dtype=jnp.int32)
    earlier_rows = (row_ids[:, None] > row_ids[None, :]).astype(jnp.bfloat16)
    every_row = jnp.ones((tok_count,), dtype=bool)
    one_hot = ((target[:, None] == peer_ids[None, :]) & every_row[:, None]).astype(jnp.bfloat16)
    before = jnp.dot(earlier_rows, one_hot, preferred_element_type=jnp.float32)
    buffer_index = target * capacity + jnp.sum(before * one_hot.astype(jnp.float32), axis=1).astype(
        jnp.int32
    )
    slot_block = jnp.zeros((tok_count, head_width), jnp.bfloat16).at[:, 0].set(
        local_slot.astype(jnp.bfloat16)
    )
    payload = jnp.concatenate([query, values, head_grad, slot_block], axis=1)
    buffer_ids = jnp.arange(peer_count * capacity, dtype=jnp.int32)
    to_buffer = (buffer_ids[:, None] == buffer_index[None, :]).astype(jnp.bfloat16)
    send_rows = jnp.dot(to_buffer, payload, preferred_element_type=jnp.float32).astype(jnp.bfloat16)
    empty = (buffer_ids[:, None] * 0 + jnp.arange(head_width)[None, :]) == 0
    used = jnp.sum(to_buffer.astype(jnp.float32), axis=1) > 0
    send_rows = send_rows.at[:, 3 * head_width :].set(
        jnp.where(
            empty & ~used[:, None],
            jnp.bfloat16(tok_count),
            send_rows[:, 3 * head_width :],
        )
    )
    recv_rows = lax.all_to_all(send_rows, SEQ, split_axis=0, concat_axis=0, tiled=True)
    recv_slots = recv_rows[:, 3 * head_width].astype(jnp.int32)
    to_sorted = (row_ids[:, None] == recv_slots[None, :]).astype(jnp.bfloat16)
    sorted_rows = jnp.dot(
        to_sorted, recv_rows[:, : 3 * head_width], preferred_element_type=jnp.float32
    ).astype(jnp.bfloat16)
    halo_rows = shifted(sorted_rows[tail_start:, : 2 * head_width], SEQ, 1)
    sorted_query = sorted_rows[:, :head_width]
    own_keys = unit_keys(sorted_query).reshape(group_count, GROUP, head_width)
    halo_keys = unit_keys(halo_rows[:, :head_width])
    q_blocks = sorted_query.reshape(group_count, GROUP, head_width)
    v_blocks = sorted_rows[:, head_width : 2 * head_width].reshape(group_count, GROUP, head_width)
    g_blocks = sorted_rows[:, 2 * head_width :].reshape(group_count, GROUP, head_width)
    prev_keys = jnp.concatenate([halo_keys[None], own_keys[:-1]], axis=0)
    prev_values = jnp.concatenate([halo_rows[None, :, head_width:], v_blocks[:-1]], axis=0)
    key_window = jnp.concatenate([own_keys, prev_keys], axis=1)
    value_window = jnp.concatenate([v_blocks, prev_values], axis=1)
    scores = (
        jnp.einsum("cqd,ckd->cqk", q_blocks, key_window, preferred_element_type=jnp.float32)
        * scale_factor
    )
    self_mask = jnp.arange(GROUP)[:, None] == jnp.arange(2 * GROUP)[None, :]
    scores = jnp.where(self_mask[None], masked_score, scores)
    probs = jax.nn.softmax(scores, axis=-1)
    dprob = jnp.einsum("cqd,ckd->cqk", g_blocks, value_window, preferred_element_type=jnp.float32)
    dscore = probs * (dprob - jnp.sum(probs * dprob, axis=-1, keepdims=True))
    probs_low = probs.astype(jnp.bfloat16)
    dscore_low = dscore.astype(jnp.bfloat16)
    dquery = (
        jnp.einsum("cqk,ckd->cqd", dscore_low, key_window, preferred_element_type=jnp.float32)
        * scale_factor
    )
    dkey_window = (
        jnp.einsum("cqk,cqd->ckd", dscore_low, q_blocks, preferred_element_type=jnp.float32)
        * scale_factor
    )
    dvalue_window = jnp.einsum(
        "cqk,cqd->ckd", probs_low, g_blocks, preferred_element_type=jnp.float32
    )
    grad_window = jnp.concatenate([dkey_window, dvalue_window], axis=-1)
    own_part = grad_window[:, :GROUP]
    later_part = grad_window[1:, GROUP:]
    outgoing = grad_window[0, GROUP:]
    incoming = shifted(outgoing, SEQ, -1)
    key_value = (own_part + jnp.concatenate([later_part, incoming[None]], axis=0)).reshape(
        tok_count, 2 * head_width
    )
    dquery_s = dquery.reshape(tok_count, head_width)
    dkey_s = key_value[:, :head_width]
    dvalue_s = key_value[:, head_width:]
    query_float = sorted_query.astype(jnp.float32)
    norm_s = jnp.sqrt(jnp.sum(query_float * query_float, axis=1, keepdims=True) + eps_norm)
    along = jnp.sum(query_float * dkey_s, axis=1, keepdims=True)
    dshared_s = dquery_s + dkey_s / norm_s - query_float * (along / norm_s**3)
    sorted_grads = jnp.concatenate(
        [dshared_s.astype(jnp.bfloat16), dvalue_s.astype(jnp.bfloat16)], axis=1
    )
    return_rows = lax.dot_general(
        to_sorted, sorted_grads, (((0,), (0,)), ((), ())), preferred_element_type=jnp.float32
    ).astype(jnp.bfloat16)
    nz, ny, nc = (lax.axis_size(a) for a in SEQ)
    my_core = lax.axis_index("c")
    by_peer = return_rows.reshape(peer_count, capacity, 2 * head_width)
    by_chip = by_peer.reshape(peer_count // nc, nc, capacity, 2 * head_width)
    to_chip = jnp.stack([jnp.roll(by_chip, -j, axis=1) for j in range(nc)], axis=2).reshape(
        peer_count, nc, capacity, 2 * head_width
    )
    back_rows = lax.all_to_all(to_chip, SEQ, split_axis=0, concat_axis=0, tiled=True)
    rows = feat_count // (nz * ny * nc)
    blocks = whole.reshape(tok_count, nz, ny, nc, rows).transpose(3, 0, 1, 2, 4)
    shares = blocks.reshape(nc, tok_count, ny * nz * rows)
    index_block = jnp.zeros((tok_count, head_width), jnp.bfloat16).at[:, 0].set(
        buffer_index.astype(jnp.bfloat16)
    )
    outgoing_shares = jnp.concatenate(
        [shares, jnp.broadcast_to(index_block[None], (nc, tok_count, head_width))], axis=2
    )
    chip_shares = lax.all_to_all(outgoing_shares, "c", 0, 0, tiled=True)
    grads = jnp.zeros((ny * nz * rows, 2 * head_width), jnp.float32)
    for source in range(nc):
        offset = (source - my_core) % nc
        rows_in = jnp.take(back_rows, offset, axis=1).reshape(peer_count * capacity, 2 * head_width)
        source_index = chip_shares[source, :, ny * nz * rows].astype(jnp.int32)
        source_buffer = (buffer_ids[:, None] == source_index[None, :]).astype(jnp.bfloat16)
        source_grads = lax.dot_general(
            source_buffer, rows_in, (((0,), (0,)), ((), ())), preferred_element_type=jnp.float32
        ).astype(jnp.bfloat16)
        grads = grads + lax.dot_general(
            chip_shares[source, :, : ny * nz * rows],
            source_grads,
            (((0,), (0,)), ((), ())),
            preferred_element_type=jnp.float32,
        )
    grads = grads.reshape(nz * ny, rows, 2 * head_width)
    grads = jnp.sum(
        lax.all_to_all(grads.astype(jnp.bfloat16), ("z", "y"), 0, 0, tiled=True).astype(jnp.float32),
        axis=0,
    )
    grads = grads.reshape(rows, 2 * head_width)
    return (grads[:, :head_width], grads[:, head_width:])


def split_mesh(mesh):
    devices = mesh.devices
    seq_n, head_n = devices.shape
    column = devices[:, 0]
    cores = sorted({d.core_on_chip for d in column})
    ys = sorted({d.coords[1] for d in column})
    nc, ny = len(cores), len(ys)
    nz = seq_n // (nc * ny)
    grid = devices.reshape(nz, ny, nc, head_n)
    for z in range(nz):
        for y in range(ny):
            for c in range(nc):
                d = grid[z, y, c, 0]
                assert d.core_on_chip == cores[c] and d.coords[1] == ys[y]
    return Mesh(grid, SEQ + ("head",))


def solution(mesh):
    fine = split_mesh(mesh)
    in_specs = (
        P(SEQ, "head"),
        P(None, "head"),
        P(None, "head"),
        P(SEQ, "head"),
        P("head", SEQ),
    )
    out_specs = (P(SEQ, "head"), P(SEQ, "head"))
    return jax.shard_map(
        per_device, mesh=fine, in_specs=in_specs, out_specs=out_specs, check_vma=False
    )
```

```python
import math

import jax
import jax.numpy as jnp
from jax import lax
from jax.sharding import Mesh
from jax.sharding import PartitionSpec as P

GROUP = 64

SEQ = ("z", "y", "c")


eps_norm = 1e-06
masked_score = -1000000000.0


def shifted(value, axis, steps):
    count = lax.axis_size(axis)
    pairs = [(source, (source + steps) % count) for source in range(count)]
    return lax.ppermute(value, axis, pairs)


def unit_keys(block):
    block_float = block.astype(jnp.float32)
    norm_rows = jnp.sqrt(jnp.sum(block_float * block_float, axis=1, keepdims=True) + eps_norm)
    return (block_float / norm_rows).astype(jnp.bfloat16)


def per_device(tokens, shared_weight, value_weight, head_grad, sorted_slot):
    tok_count = tokens.shape[0]
    head_n = lax.axis_size("head")
    spread = jnp.broadcast_to(tokens[None], (head_n,) + tokens.shape)
    gathered = lax.all_to_all(spread, "head", 0, 0, tiled=True)
    whole = gathered.transpose(1, 0, 2).reshape(tok_count, head_n * tokens.shape[1])
    feat_count = whole.shape[1]
    head_width = shared_weight.shape[1]
    peer_count = lax.axis_size(SEQ)
    capacity = 2 * tok_count // peer_count
    group_count = tok_count // GROUP
    tail_start = tok_count - GROUP
    scale_factor = 1.0 / math.sqrt(head_width)
    query = jnp.dot(whole, shared_weight, preferred_element_type=jnp.float32).astype(jnp.bfloat16)
    values = jnp.dot(whole, value_weight, preferred_element_type=jnp.float32).astype(jnp.bfloat16)
    slot_ids = sorted_slot[0]
    target = slot_ids // tok_count
    local_slot = slot_ids - target * tok_count
    peer_ids = jnp.arange(peer_count, dtype=jnp.int32)
    row_ids = jnp.arange(tok_count, dtype=jnp.int32)
    earlier_rows = (row_ids[:, None] > row_ids[None, :]).astype(jnp.bfloat16)
    every_row = jnp.ones((tok_count,), dtype=bool)
    one_hot = ((target[:, None] == peer_ids[None, :]) & every_row[:, None]).astype(jnp.bfloat16)
    before = jnp.dot(earlier_rows, one_hot, preferred_element_type=jnp.float32)
    buffer_index = target * capacity + jnp.sum(before * one_hot.astype(jnp.float32), axis=1).astype(
        jnp.int32
    )
    is_tail = local_slot >= tail_start
    tail_hot = one_hot * is_tail[:, None].astype(jnp.bfloat16)
    before_tail = jnp.dot(earlier_rows, tail_hot, preferred_element_type=jnp.float32)
    tail_rank = jnp.sum(before_tail * one_hot.astype(jnp.float32), axis=1).astype(jnp.int32)
    lanes = 2 * capacity
    main_slot = target * lanes + buffer_index % capacity
    next_slot = ((target + 1) % peer_count) * lanes + capacity + tail_rank
    window = GROUP + tok_count
    main_index = jnp.zeros((tok_count, head_width), jnp.bfloat16).at[:, 0].set(
        (local_slot + GROUP).astype(jnp.bfloat16)
    )
    next_index = jnp.zeros((tok_count, head_width), jnp.bfloat16).at[:, 0].set(
        (local_slot - tail_start).astype(jnp.bfloat16)
    )
    rows_main = jnp.concatenate([query, values, head_grad, main_index], axis=1)
    rows_next = jnp.concatenate([query, values, head_grad, next_index], axis=1)
    buffer_ids = jnp.arange(peer_count * capacity, dtype=jnp.int32)
    send_ids = jnp.arange(peer_count * lanes, dtype=jnp.int32)
    to_buffer = (buffer_ids[:, None] == buffer_index[None, :]).astype(jnp.bfloat16)
    to_main = (send_ids[:, None] == main_slot[None, :]).astype(jnp.bfloat16)
    to_next = ((send_ids[:, None] == next_slot[None, :]) & is_tail[None, :]).astype(jnp.bfloat16)
    send_rows = (
        jnp.dot(to_main, rows_main, preferred_element_type=jnp.float32)
        + jnp.dot(to_next, rows_next, preferred_element_type=jnp.float32)
    ).astype(jnp.bfloat16)
    empty = (send_ids[:, None] * 0 + jnp.arange(head_width)[None, :]) == 0
    used = jnp.sum(to_main.astype(jnp.float32) + to_next.astype(jnp.float32), axis=1) > 0
    send_rows = send_rows.at[:, 3 * head_width :].set(
        jnp.where(
            empty & ~used[:, None],
            jnp.bfloat16(window),
            send_rows[:, 3 * head_width :],
        )
    )
    recv_rows = lax.all_to_all(send_rows, SEQ, split_axis=0, concat_axis=0, tiled=True)
    recv_index = recv_rows[:, 3 * head_width].astype(jnp.int32)
    window_ids = jnp.arange(window, dtype=jnp.int32)
    to_window = (window_ids[:, None] == recv_index[None, :]).astype(jnp.bfloat16)
    window_rows = jnp.dot(
        to_window, recv_rows[:, : 3 * head_width], preferred_element_type=jnp.float32
    ).astype(jnp.bfloat16)
    halo_rows = window_rows[:GROUP, : 2 * head_width]
    sorted_rows = window_rows[GROUP:]
    recv_main = recv_index.reshape(peer_count, lanes)[:, :capacity].reshape(-1) - GROUP
    to_sorted = (row_ids[:, None] == recv_main[None, :]).astype(jnp.bfloat16)
    sorted_query = sorted_rows[:, :head_width]
    own_keys = unit_keys(sorted_query).reshape(group_count, GROUP, head_width)
    halo_keys = unit_keys(halo_rows[:, :head_width])
    q_blocks = sorted_query.reshape(group_count, GROUP, head_width)
    v_blocks = sorted_rows[:, head_width : 2 * head_width].reshape(group_count, GROUP, head_width)
    g_blocks = sorted_rows[:, 2 * head_width :].reshape(group_count, GROUP, head_width)
    prev_keys = jnp.concatenate([halo_keys[None], own_keys[:-1]], axis=0)
    prev_values = jnp.concatenate([halo_rows[None, :, head_width:], v_blocks[:-1]], axis=0)
    key_window = jnp.concatenate([own_keys, prev_keys], axis=1)
    value_window = jnp.concatenate([v_blocks, prev_values], axis=1)
    scores = (
        jnp.einsum("cqd,ckd->cqk", q_blocks, key_window, preferred_element_type=jnp.float32)
        * scale_factor
    )
    self_mask = jnp.arange(GROUP)[:, None] == jnp.arange(2 * GROUP)[None, :]
    scores = jnp.where(self_mask[None], masked_score, scores)
    probs = jax.nn.softmax(scores, axis=-1)
    dprob = jnp.einsum("cqd,ckd->cqk", g_blocks, value_window, preferred_element_type=jnp.float32)
    dscore = probs * (dprob - jnp.sum(probs * dprob, axis=-1, keepdims=True))
    probs_low = probs.astype(jnp.bfloat16)
    dscore_low = dscore.astype(jnp.bfloat16)
    dquery = (
        jnp.einsum("cqk,ckd->cqd", dscore_low, key_window, preferred_element_type=jnp.float32)
        * scale_factor
    )
    dkey_window = (
        jnp.einsum("cqk,cqd->ckd", dscore_low, q_blocks, preferred_element_type=jnp.float32)
        * scale_factor
    )
    dvalue_window = jnp.einsum(
        "cqk,cqd->ckd", probs_low, g_blocks, preferred_element_type=jnp.float32
    )
    grad_window = jnp.concatenate([dkey_window, dvalue_window], axis=-1)
    own_part = grad_window[:, :GROUP]
    later_part = grad_window[1:, GROUP:]
    outgoing = grad_window[0, GROUP:]
    incoming = shifted(outgoing, SEQ, -1)
    key_value = (own_part + jnp.concatenate([later_part, incoming[None]], axis=0)).reshape(
        tok_count, 2 * head_width
    )
    dquery_s = dquery.reshape(tok_count, head_width)
    dkey_s = key_value[:, :head_width]
    dvalue_s = key_value[:, head_width:]
    query_float = sorted_query.astype(jnp.float32)
    norm_s = jnp.sqrt(jnp.sum(query_float * query_float, axis=1, keepdims=True) + eps_norm)
    along = jnp.sum(query_float * dkey_s, axis=1, keepdims=True)
    dshared_s = dquery_s + dkey_s / norm_s - query_float * (along / norm_s**3)
    sorted_grads = jnp.concatenate(
        [dshared_s.astype(jnp.bfloat16), dvalue_s.astype(jnp.bfloat16)], axis=1
    )
    return_rows = lax.dot_general(
        to_sorted, sorted_grads, (((0,), (0,)), ((), ())), preferred_element_type=jnp.float32
    ).astype(jnp.bfloat16)
    nz, ny, nc = (lax.axis_size(a) for a in SEQ)
    my_core = lax.axis_index("c")
    by_peer = return_rows.reshape(peer_count, capacity, 2 * head_width)
    by_chip = by_peer.reshape(peer_count // nc, nc, capacity, 2 * head_width)
    to_chip = jnp.stack([jnp.roll(by_chip, -j, axis=1) for j in range(nc)], axis=2).reshape(
        peer_count, nc, capacity, 2 * head_width
    )
    back_rows = lax.all_to_all(to_chip, SEQ, split_axis=0, concat_axis=0, tiled=True)
    rows = feat_count // (nz * ny * nc)
    blocks = whole.reshape(tok_count, nz, ny, nc, rows).transpose(3, 0, 1, 2, 4)
    shares = blocks.reshape(nc, tok_count, ny * nz * rows)
    index_block = jnp.zeros((tok_count, head_width), jnp.bfloat16).at[:, 0].set(
        buffer_index.astype(jnp.bfloat16)
    )
    outgoing_shares = jnp.concatenate(
        [shares, jnp.broadcast_to(index_block[None], (nc, tok_count, head_width))], axis=2
    )
    chip_shares = lax.all_to_all(outgoing_shares, "c", 0, 0, tiled=True)
    grads = jnp.zeros((ny * nz * rows, 2 * head_width), jnp.float32)
    for source in range(nc):
        offset = (source - my_core) % nc
        rows_in = jnp.take(back_rows, offset, axis=1).reshape(peer_count * capacity, 2 * head_width)
        source_index = chip_shares[source, :, ny * nz * rows].astype(jnp.int32)
        source_buffer = (buffer_ids[:, None] == source_index[None, :]).astype(jnp.bfloat16)
        source_grads = lax.dot_general(
            source_buffer, rows_in, (((0,), (0,)), ((), ())), preferred_element_type=jnp.float32
        ).astype(jnp.bfloat16)
        grads = grads + lax.dot_general(
            chip_shares[source, :, : ny * nz * rows],
            source_grads,
            (((0,), (0,)), ((), ())),
            preferred_element_type=jnp.float32,
        )
    grads = grads.reshape(nz * ny, rows, 2 * head_width)
    grads = jnp.sum(
        lax.all_to_all(grads.astype(jnp.bfloat16), ("z", "y"), 0, 0, tiled=True).astype(jnp.float32),
        axis=0,
    )
    grads = grads.reshape(rows, 2 * head_width)
    return (grads[:, :head_width], grads[:, head_width:])


def split_mesh(mesh):
    devices = mesh.devices
    seq_n, head_n = devices.shape
    column = devices[:, 0]
    cores = sorted({d.core_on_chip for d in column})
    ys = sorted({d.coords[1] for d in column})
    nc, ny = len(cores), len(ys)
    nz = seq_n // (nc * ny)
    grid = devices.reshape(nz, ny, nc, head_n)
    for z in range(nz):
        for y in range(ny):
            for c in range(nc):
                d = grid[z, y, c, 0]
                assert d.core_on_chip == cores[c] and d.coords[1] == ys[y]
    return Mesh(grid, SEQ + ("head",))


def solution(mesh):
    fine = split_mesh(mesh)
    in_specs = (
        P(SEQ, "head"),
        P(None, "head"),
        P(None, "head"),
        P(SEQ, "head"),
        P("head", SEQ),
    )
    out_specs = (P(SEQ, "head"), P(SEQ, "head"))
    return jax.shard_map(
        per_device, mesh=fine, in_specs=in_specs, out_specs=out_specs, check_vma=False
    )
```

```python
import math

import jax
import jax.numpy as jnp
from jax import lax
from jax.sharding import Mesh
from jax.sharding import PartitionSpec as P

GROUP = 64

SEQ = ("z", "y", "c")


eps_norm = 1e-06
masked_score = -1000000000.0


def shifted(value, axis, steps):
    count = lax.axis_size(axis)
    pairs = [(source, (source + steps) % count) for source in range(count)]
    return lax.ppermute(value, axis, pairs)


def unit_keys(block):
    block_float = block.astype(jnp.float32)
    norm_rows = jnp.sqrt(jnp.sum(block_float * block_float, axis=1, keepdims=True) + eps_norm)
    return (block_float / norm_rows).astype(jnp.bfloat16)


def per_device(tokens, shared_weight, value_weight, head_grad, sorted_slot):
    tok_count = tokens.shape[0]
    head_n = lax.axis_size("head")
    spread = jnp.broadcast_to(tokens[None], (head_n,) + tokens.shape)
    gathered = lax.all_to_all(spread, "head", 0, 0, tiled=True)
    whole = gathered.transpose(1, 0, 2).reshape(tok_count, head_n * tokens.shape[1])
    feat_count = whole.shape[1]
    head_width = shared_weight.shape[1]
    peer_count = lax.axis_size(SEQ)
    capacity = 2 * tok_count // peer_count
    group_count = tok_count // GROUP
    tail_start = tok_count - GROUP
    scale_factor = 1.0 / math.sqrt(head_width)
    query = jnp.dot(whole, shared_weight, preferred_element_type=jnp.float32).astype(jnp.bfloat16)
    values = jnp.dot(whole, value_weight, preferred_element_type=jnp.float32).astype(jnp.bfloat16)
    slot_ids = sorted_slot[0]
    target = slot_ids // tok_count
    local_slot = slot_ids - target * tok_count
    peer_ids = jnp.arange(peer_count, dtype=jnp.int32)
    row_ids = jnp.arange(tok_count, dtype=jnp.int32)
    earlier_rows = (row_ids[:, None] > row_ids[None, :]).astype(jnp.bfloat16)
    every_row = jnp.ones((tok_count,), dtype=bool)
    one_hot = ((target[:, None] == peer_ids[None, :]) & every_row[:, None]).astype(jnp.bfloat16)
    before = jnp.dot(earlier_rows, one_hot, preferred_element_type=jnp.float32)
    buffer_index = target * capacity + jnp.sum(before * one_hot.astype(jnp.float32), axis=1).astype(
        jnp.int32
    )
    slot_block = jnp.zeros((tok_count, head_width), jnp.bfloat16).at[:, 0].set(
        local_slot.astype(jnp.bfloat16)
    )
    payload = jnp.concatenate([query, values, head_grad, slot_block], axis=1)
    buffer_ids = jnp.arange(peer_count * capacity, dtype=jnp.int32)
    to_buffer = (buffer_ids[:, None] == buffer_index[None, :]).astype(jnp.bfloat16)
    send_rows = jnp.dot(to_buffer, payload, preferred_element_type=jnp.float32).astype(jnp.bfloat16)
    empty = (buffer_ids[:, None] * 0 + jnp.arange(head_width)[None, :]) == 0
    used = jnp.sum(to_buffer.astype(jnp.float32), axis=1) > 0
    send_rows = send_rows.at[:, 3 * head_width :].set(
        jnp.where(
            empty & ~used[:, None],
            jnp.bfloat16(tok_count),
            send_rows[:, 3 * head_width :],
        )
    )
    recv_rows = lax.all_to_all(send_rows, SEQ, split_axis=0, concat_axis=0, tiled=True)
    recv_slots = recv_rows[:, 3 * head_width].astype(jnp.int32)
    to_sorted = (row_ids[:, None] == recv_slots[None, :]).astype(jnp.bfloat16)
    sorted_rows = jnp.dot(
        to_sorted, recv_rows[:, : 3 * head_width], preferred_element_type=jnp.float32
    ).astype(jnp.bfloat16)
    halo_rows = shifted(sorted_rows[tail_start:, : 2 * head_width], SEQ, 1)
    sorted_query = sorted_rows[:, :head_width]
    own_keys = unit_keys(sorted_query).reshape(group_count, GROUP, head_width)
    halo_keys = unit_keys(halo_rows[:, :head_width])
    q_blocks = sorted_query.reshape(group_count, GROUP, head_width)
    v_blocks = sorted_rows[:, head_width : 2 * head_width].reshape(group_count, GROUP, head_width)
    g_blocks = sorted_rows[:, 2 * head_width :].reshape(group_count, GROUP, head_width)
    prev_keys = jnp.concatenate([halo_keys[None], own_keys[:-1]], axis=0)
    prev_values = jnp.concatenate([halo_rows[None, :, head_width:], v_blocks[:-1]], axis=0)
    key_window = jnp.concatenate([own_keys, prev_keys], axis=1)
    value_window = jnp.concatenate([v_blocks, prev_values], axis=1)
    scores = (
        jnp.einsum("cqd,ckd->cqk", q_blocks, key_window, preferred_element_type=jnp.float32)
        * scale_factor
    )
    self_mask = jnp.arange(GROUP)[:, None] == jnp.arange(2 * GROUP)[None, :]
    scores = jnp.where(self_mask[None], masked_score, scores)
    probs = jax.nn.softmax(scores, axis=-1)
    dprob = jnp.einsum("cqd,ckd->cqk", g_blocks, value_window, preferred_element_type=jnp.float32)
    dscore = probs * (dprob - jnp.sum(probs * dprob, axis=-1, keepdims=True))
    probs_low = probs.astype(jnp.bfloat16)
    dscore_low = dscore.astype(jnp.bfloat16)
    dquery = (
        jnp.einsum("cqk,ckd->cqd", dscore_low, key_window, preferred_element_type=jnp.float32)
        * scale_factor
    )
    dkey_window = (
        jnp.einsum("cqk,cqd->ckd", dscore_low, q_blocks, preferred_element_type=jnp.float32)
        * scale_factor
    )
    dvalue_window = jnp.einsum(
        "cqk,cqd->ckd", probs_low, g_blocks, preferred_element_type=jnp.float32
    )
    grad_window = jnp.concatenate([dkey_window, dvalue_window], axis=-1)
    own_part = grad_window[:, :GROUP]
    later_part = grad_window[1:, GROUP:]
    outgoing = grad_window[0, GROUP:]
    incoming = shifted(outgoing, SEQ, -1)
    key_value = (own_part + jnp.concatenate([later_part, incoming[None]], axis=0)).reshape(
        tok_count, 2 * head_width
    )
    dquery_s = dquery.reshape(tok_count, head_width)
    dkey_s = key_value[:, :head_width]
    dvalue_s = key_value[:, head_width:]
    query_float = sorted_query.astype(jnp.float32)
    norm_s = jnp.sqrt(jnp.sum(query_float * query_float, axis=1, keepdims=True) + eps_norm)
    along = jnp.sum(query_float * dkey_s, axis=1, keepdims=True)
    dshared_s = dquery_s + dkey_s / norm_s - query_float * (along / norm_s**3)
    sorted_grads = jnp.concatenate(
        [dshared_s.astype(jnp.bfloat16), dvalue_s.astype(jnp.bfloat16)], axis=1
    )
    nz, ny, nc = (lax.axis_size(a) for a in SEQ)
    my_core = lax.axis_index("c")
    slot_chip = recv_slots.reshape(peer_count // nc, nc, capacity)
    fanned = jnp.stack([jnp.roll(slot_chip, -j, axis=1) for j in range(nc)], axis=2).reshape(-1)
    to_fanned = (row_ids[:, None] == fanned[None, :]).astype(jnp.bfloat16)
    to_chip = (
        lax.dot_general(
            to_fanned, sorted_grads, (((0,), (0,)), ((), ())), preferred_element_type=jnp.float32
        )
        .astype(jnp.bfloat16)
        .reshape(peer_count, nc, capacity, 2 * head_width)
    )
    back_rows = lax.all_to_all(to_chip, SEQ, split_axis=0, concat_axis=0, tiled=True)
    rows = feat_count // (nz * ny * nc)
    blocks = whole.reshape(tok_count, nz, ny, nc, rows).transpose(3, 0, 1, 2, 4)
    shares = blocks.reshape(nc, tok_count, ny * nz * rows)
    index_block = jnp.zeros((tok_count, head_width), jnp.bfloat16).at[:, 0].set(
        buffer_index.astype(jnp.bfloat16)
    )
    outgoing_shares = jnp.concatenate(
        [shares, jnp.broadcast_to(index_block[None], (nc, tok_count, head_width))], axis=2
    )
    chip_shares = lax.all_to_all(outgoing_shares, "c", 0, 0, tiled=True)
    source_grads = []
    for source in range(nc):
        offset = (source - my_core) % nc
        rows_in = jnp.take(back_rows, offset, axis=1).reshape(peer_count * capacity, 2 * head_width)
        source_index = chip_shares[source, :, ny * nz * rows].astype(jnp.int32)
        source_buffer = (buffer_ids[:, None] == source_index[None, :]).astype(jnp.bfloat16)
        source_grads.append(
            lax.dot_general(
                source_buffer, rows_in, (((0,), (0,)), ((), ())), preferred_element_type=jnp.float32
            ).astype(jnp.bfloat16)
        )
    grads = lax.dot_general(
        chip_shares[:, :, : ny * nz * rows].reshape(nc * tok_count, ny * nz * rows),
        jnp.concatenate(source_grads, axis=0),
        (((0,), (0,)), ((), ())),
        preferred_element_type=jnp.float32,
    )
    grads = grads.reshape(nz * ny, rows, 2 * head_width)
    grads = jnp.sum(
        lax.all_to_all(grads.astype(jnp.bfloat16), ("z", "y"), 0, 0, tiled=True).astype(jnp.float32),
        axis=0,
    )
    grads = grads.reshape(rows, 2 * head_width)
    return (grads[:, :head_width], grads[:, head_width:])


def split_mesh(mesh):
    devices = mesh.devices
    seq_n, head_n = devices.shape
    column = devices[:, 0]
    cores = sorted({d.core_on_chip for d in column})
    ys = sorted({d.coords[1] for d in column})
    nc, ny = len(cores), len(ys)
    nz = seq_n // (nc * ny)
    grid = devices.reshape(nz, ny, nc, head_n)
    for z in range(nz):
        for y in range(ny):
            for c in range(nc):
                d = grid[z, y, c, 0]
                assert d.core_on_chip == cores[c] and d.coords[1] == ys[y]
    return Mesh(grid, SEQ + ("head",))


def solution(mesh):
    fine = split_mesh(mesh)
    in_specs = (
        P(SEQ, "head"),
        P(None, "head"),
        P(None, "head"),
        P(SEQ, "head"),
        P("head", SEQ),
    )
    out_specs = (P(SEQ, "head"), P(SEQ, "head"))
    return jax.shard_map(
        per_device, mesh=fine, in_specs=in_specs, out_specs=out_specs, check_vma=False
    )
```

```python
import math

import jax
import jax.numpy as jnp
from jax import lax
from jax.sharding import Mesh
from jax.sharding import PartitionSpec as P

GROUP = 64

SEQ = ("z", "y", "c")


eps_norm = 1e-06
masked_score = -1000000000.0


def shifted(value, axis, steps):
    count = lax.axis_size(axis)
    pairs = [(source, (source + steps) % count) for source in range(count)]
    return lax.ppermute(value, axis, pairs)


def unit_keys(block):
    block_float = block.astype(jnp.float32)
    norm_rows = jnp.sqrt(jnp.sum(block_float * block_float, axis=1, keepdims=True) + eps_norm)
    return (block_float / norm_rows).astype(jnp.bfloat16)


def per_device(tokens, shared_weight, value_weight, head_grad, sorted_slot):
    tok_count = tokens.shape[0]
    head_n = lax.axis_size("head")
    spread = jnp.broadcast_to(tokens[None], (head_n,) + tokens.shape)
    gathered = lax.all_to_all(spread, "head", 0, 0, tiled=True)
    whole = gathered.transpose(1, 0, 2).reshape(tok_count, head_n * tokens.shape[1])
    feat_count = whole.shape[1]
    head_width = shared_weight.shape[1]
    peer_count = lax.axis_size(SEQ)
    capacity = 2 * tok_count // peer_count
    group_count = tok_count // GROUP
    tail_start = tok_count - GROUP
    scale_factor = 1.0 / math.sqrt(head_width)
    query = jnp.dot(whole, shared_weight, preferred_element_type=jnp.float32).astype(jnp.bfloat16)
    values = jnp.dot(whole, value_weight, preferred_element_type=jnp.float32).astype(jnp.bfloat16)
    slot_ids = sorted_slot[0]
    target = slot_ids // tok_count
    local_slot = slot_ids - target * tok_count
    peer_ids = jnp.arange(peer_count, dtype=jnp.int32)
    row_ids = jnp.arange(tok_count, dtype=jnp.int32)
    earlier_rows = (row_ids[:, None] > row_ids[None, :]).astype(jnp.bfloat16)
    every_row = jnp.ones((tok_count,), dtype=bool)
    one_hot = ((target[:, None] == peer_ids[None, :]) & every_row[:, None]).astype(jnp.bfloat16)
    before = jnp.dot(earlier_rows, one_hot, preferred_element_type=jnp.float32)
    buffer_index = target * capacity + jnp.sum(before * one_hot.astype(jnp.float32), axis=1).astype(
        jnp.int32
    )
    slot_block = jnp.zeros((tok_count, head_width), jnp.bfloat16).at[:, 0].set(
        local_slot.astype(jnp.bfloat16)
    )
    payload = jnp.concatenate([query, values, head_grad, slot_block], axis=1)
    buffer_ids = jnp.arange(peer_count * capacity, dtype=jnp.int32)
    to_buffer = (buffer_ids[:, None] == buffer_index[None, :]).astype(jnp.bfloat16)
    send_rows = jnp.dot(to_buffer, payload, preferred_element_type=jnp.float32).astype(jnp.bfloat16)
    empty = (buffer_ids[:, None] * 0 + jnp.arange(head_width)[None, :]) == 0
    used = jnp.sum(to_buffer.astype(jnp.float32), axis=1) > 0
    send_rows = send_rows.at[:, 3 * head_width :].set(
        jnp.where(
            empty & ~used[:, None],
            jnp.bfloat16(tok_count),
            send_rows[:, 3 * head_width :],
        )
    )
    recv_rows = lax.all_to_all(send_rows, SEQ, split_axis=0, concat_axis=0, tiled=True)
    recv_slots = recv_rows[:, 3 * head_width].astype(jnp.int32)
    to_sorted = (row_ids[:, None] == recv_slots[None, :]).astype(jnp.bfloat16)
    sorted_rows = jnp.dot(
        to_sorted, recv_rows[:, : 3 * head_width], preferred_element_type=jnp.float32
    ).astype(jnp.bfloat16)
    halo_rows = shifted(sorted_rows[tail_start:, : 2 * head_width], SEQ, 1)
    sorted_query = sorted_rows[:, :head_width]
    own_keys = unit_keys(sorted_query).reshape(group_count, GROUP, head_width)
    halo_keys = unit_keys(halo_rows[:, :head_width])
    q_blocks = sorted_query.reshape(group_count, GROUP, head_width)
    v_blocks = sorted_rows[:, head_width : 2 * head_width].reshape(group_count, GROUP, head_width)
    g_blocks = sorted_rows[:, 2 * head_width :].reshape(group_count, GROUP, head_width)
    prev_keys = jnp.concatenate([halo_keys[None], own_keys[:-1]], axis=0)
    prev_values = jnp.concatenate([halo_rows[None, :, head_width:], v_blocks[:-1]], axis=0)
    key_window = jnp.concatenate([own_keys, prev_keys], axis=1)
    value_window = jnp.concatenate([v_blocks, prev_values], axis=1)
    scores = (
        jnp.einsum("cqd,ckd->cqk", q_blocks, key_window, preferred_element_type=jnp.float32)
        * scale_factor
    )
    self_mask = jnp.arange(GROUP)[:, None] == jnp.arange(2 * GROUP)[None, :]
    scores = jnp.where(self_mask[None], masked_score, scores)
    probs = jax.nn.softmax(scores, axis=-1)
    dprob = jnp.einsum("cqd,ckd->cqk", g_blocks, value_window, preferred_element_type=jnp.float32)
    dscore = probs * (dprob - jnp.sum(probs * dprob, axis=-1, keepdims=True))
    probs_low = probs.astype(jnp.bfloat16)
    dscore_low = dscore.astype(jnp.bfloat16)
    dquery = (
        jnp.einsum("cqk,ckd->cqd", dscore_low, key_window, preferred_element_type=jnp.float32)
        * scale_factor
    )
    dkey_window = (
        jnp.einsum("cqk,cqd->ckd", dscore_low, q_blocks, preferred_element_type=jnp.float32)
        * scale_factor
    )
    dvalue_window = jnp.einsum(
        "cqk,cqd->ckd", probs_low, g_blocks, preferred_element_type=jnp.float32
    )
    grad_window = jnp.concatenate([dkey_window, dvalue_window], axis=-1)
    own_part = grad_window[:, :GROUP]
    later_part = grad_window[1:, GROUP:]
    outgoing = grad_window[0, GROUP:]
    incoming = shifted(outgoing, SEQ, -1)
    key_value = (own_part + jnp.concatenate([later_part, incoming[None]], axis=0)).reshape(
        tok_count, 2 * head_width
    )
    dquery_s = dquery.reshape(tok_count, head_width)
    dkey_s = key_value[:, :head_width]
    dvalue_s = key_value[:, head_width:]
    query_float = sorted_query.astype(jnp.float32)
    norm_s = jnp.sqrt(jnp.sum(query_float * query_float, axis=1, keepdims=True) + eps_norm)
    along = jnp.sum(query_float * dkey_s, axis=1, keepdims=True)
    dshared_s = dquery_s + dkey_s / norm_s - query_float * (along / norm_s**3)
    sorted_grads = jnp.concatenate(
        [dshared_s.astype(jnp.bfloat16), dvalue_s.astype(jnp.bfloat16)], axis=1
    )
    nz, ny, nc = (lax.axis_size(a) for a in SEQ)
    my_core = lax.axis_index("c")
    slot_chip = recv_slots.reshape(peer_count // nc, nc, capacity)
    fanned = jnp.stack([jnp.roll(slot_chip, -j, axis=1) for j in range(nc)], axis=2).reshape(-1)
    to_fanned = (row_ids[:, None] == fanned[None, :]).astype(jnp.bfloat16)
    to_chip = (
        lax.dot_general(
            to_fanned, sorted_grads, (((0,), (0,)), ((), ())), preferred_element_type=jnp.float32
        )
        .astype(jnp.bfloat16)
        .reshape(peer_count, nc, capacity, 2 * head_width)
    )
    back_rows = lax.all_to_all(to_chip, SEQ, split_axis=0, concat_axis=0, tiled=True)
    rows = feat_count // (nz * ny * nc)
    blocks = whole.reshape(tok_count, nz, ny, nc, rows).transpose(3, 0, 1, 2, 4)
    shares = blocks.reshape(nc, tok_count, ny * nz * rows)
    index_block = jnp.zeros((tok_count, head_width), jnp.bfloat16).at[:, 0].set(
        buffer_index.astype(jnp.bfloat16)
    )
    outgoing_shares = jnp.concatenate(
        [shares, jnp.broadcast_to(index_block[None], (nc, tok_count, head_width))], axis=2
    )
    got_shares = []
    source_grads = []
    for j in range(nc):
        mine = jnp.take(outgoing_shares, (my_core + j) % nc, axis=0)
        got = mine if j == 0 else shifted(mine, "c", j)
        got_shares.append(got[:, : ny * nz * rows])
        rows_in = back_rows[:, (-j) % nc].reshape(peer_count * capacity, 2 * head_width)
        source_index = got[:, ny * nz * rows].astype(jnp.int32)
        source_buffer = (buffer_ids[:, None] == source_index[None, :]).astype(jnp.bfloat16)
        source_grads.append(
            lax.dot_general(
                source_buffer, rows_in, (((0,), (0,)), ((), ())), preferred_element_type=jnp.float32
            ).astype(jnp.bfloat16)
        )
    grads = lax.dot_general(
        jnp.concatenate(got_shares, axis=0),
        jnp.concatenate(source_grads, axis=0),
        (((0,), (0,)), ((), ())),
        preferred_element_type=jnp.float32,
    )
    grads = grads.reshape(nz * ny, rows, 2 * head_width)
    grads = jnp.sum(
        lax.all_to_all(grads.astype(jnp.bfloat16), ("z", "y"), 0, 0, tiled=True).astype(jnp.float32),
        axis=0,
    )
    grads = grads.reshape(rows, 2 * head_width)
    return (grads[:, :head_width], grads[:, head_width:])


def split_mesh(mesh):
    devices = mesh.devices
    seq_n, head_n = devices.shape
    column = devices[:, 0]
    cores = sorted({d.core_on_chip for d in column})
    ys = sorted({d.coords[1] for d in column})
    nc, ny = len(cores), len(ys)
    nz = seq_n // (nc * ny)
    grid = devices.reshape(nz, ny, nc, head_n)
    for z in range(nz):
        for y in range(ny):
            for c in range(nc):
                d = grid[z, y, c, 0]
                assert d.core_on_chip == cores[c] and d.coords[1] == ys[y]
    return Mesh(grid, SEQ + ("head",))


def solution(mesh):
    fine = split_mesh(mesh)
    in_specs = (
        P(SEQ, "head"),
        P(None, "head"),
        P(None, "head"),
        P(SEQ, "head"),
        P("head", SEQ),
    )
    out_specs = (P(SEQ, "head"), P(SEQ, "head"))
    return jax.shard_map(
        per_device, mesh=fine, in_specs=in_specs, out_specs=out_specs, check_vma=False
    )
```

```python
import math

import jax
import jax.numpy as jnp
from jax import lax
from jax.sharding import Mesh
from jax.sharding import PartitionSpec as P

GROUP = 64

SEQ = ("z", "y", "c")


eps_norm = 1e-06
masked_score = -1000000000.0


def shifted(value, axis, steps):
    count = lax.axis_size(axis)
    pairs = [(source, (source + steps) % count) for source in range(count)]
    return lax.ppermute(value, axis, pairs)


def unit_keys(block):
    block_float = block.astype(jnp.float32)
    norm_rows = jnp.sqrt(jnp.sum(block_float * block_float, axis=1, keepdims=True) + eps_norm)
    return (block_float / norm_rows).astype(jnp.bfloat16)


def per_device(tokens, shared_weight, value_weight, head_grad, sorted_slot):
    tok_count = tokens.shape[0]
    head_n = lax.axis_size("head")
    me_head = lax.axis_index("head")
    parts = jnp.stack([tokens] + [shifted(tokens, "head", j) for j in range(1, head_n)])
    gathered = jnp.take(parts, (me_head - jnp.arange(head_n)) % head_n, axis=0)
    whole = gathered.transpose(1, 0, 2).reshape(tok_count, head_n * tokens.shape[1])
    feat_count = whole.shape[1]
    head_width = shared_weight.shape[1]
    peer_count = lax.axis_size(SEQ)
    capacity = 2 * tok_count // peer_count
    group_count = tok_count // GROUP
    tail_start = tok_count - GROUP
    scale_factor = 1.0 / math.sqrt(head_width)
    query = jnp.dot(whole, shared_weight, preferred_element_type=jnp.float32).astype(jnp.bfloat16)
    values = jnp.dot(whole, value_weight, preferred_element_type=jnp.float32).astype(jnp.bfloat16)
    slot_ids = sorted_slot[0]
    target = slot_ids // tok_count
    local_slot = slot_ids - target * tok_count
    peer_ids = jnp.arange(peer_count, dtype=jnp.int32)
    row_ids = jnp.arange(tok_count, dtype=jnp.int32)
    earlier_rows = (row_ids[:, None] > row_ids[None, :]).astype(jnp.bfloat16)
    every_row = jnp.ones((tok_count,), dtype=bool)
    one_hot = ((target[:, None] == peer_ids[None, :]) & every_row[:, None]).astype(jnp.bfloat16)
    before = jnp.dot(earlier_rows, one_hot, preferred_element_type=jnp.float32)
    buffer_index = target * capacity + jnp.sum(before * one_hot.astype(jnp.float32), axis=1).astype(
        jnp.int32
    )
    slot_block = jnp.zeros((tok_count, head_width), jnp.bfloat16).at[:, 0].set(
        local_slot.astype(jnp.bfloat16)
    )
    payload = jnp.concatenate([query, values, head_grad, slot_block], axis=1)
    buffer_ids = jnp.arange(peer_count * capacity, dtype=jnp.int32)
    to_buffer = (buffer_ids[:, None] == buffer_index[None, :]).astype(jnp.bfloat16)
    send_rows = jnp.dot(to_buffer, payload, preferred_element_type=jnp.float32).astype(jnp.bfloat16)
    empty = (buffer_ids[:, None] * 0 + jnp.arange(head_width)[None, :]) == 0
    used = jnp.sum(to_buffer.astype(jnp.float32), axis=1) > 0
    send_rows = send_rows.at[:, 3 * head_width :].set(
        jnp.where(
            empty & ~used[:, None],
            jnp.bfloat16(tok_count),
            send_rows[:, 3 * head_width :],
        )
    )
    recv_rows = lax.all_to_all(send_rows, SEQ, split_axis=0, concat_axis=0, tiled=True)
    recv_slots = recv_rows[:, 3 * head_width].astype(jnp.int32)
    to_sorted = (row_ids[:, None] == recv_slots[None, :]).astype(jnp.bfloat16)
    sorted_rows = jnp.dot(
        to_sorted, recv_rows[:, : 3 * head_width], preferred_element_type=jnp.float32
    ).astype(jnp.bfloat16)
    halo_rows = shifted(sorted_rows[tail_start:, : 2 * head_width], SEQ, 1)
    sorted_query = sorted_rows[:, :head_width]
    own_keys = unit_keys(sorted_query).reshape(group_count, GROUP, head_width)
    halo_keys = unit_keys(halo_rows[:, :head_width])
    q_blocks = sorted_query.reshape(group_count, GROUP, head_width)
    v_blocks = sorted_rows[:, head_width : 2 * head_width].reshape(group_count, GROUP, head_width)
    g_blocks = sorted_rows[:, 2 * head_width :].reshape(group_count, GROUP, head_width)
    prev_keys = jnp.concatenate([halo_keys[None], own_keys[:-1]], axis=0)
    prev_values = jnp.concatenate([halo_rows[None, :, head_width:], v_blocks[:-1]], axis=0)
    key_window = jnp.concatenate([own_keys, prev_keys], axis=1)
    value_window = jnp.concatenate([v_blocks, prev_values], axis=1)
    scores = (
        jnp.einsum("cqd,ckd->cqk", q_blocks, key_window, preferred_element_type=jnp.float32)
        * scale_factor
    )
    self_mask = jnp.arange(GROUP)[:, None] == jnp.arange(2 * GROUP)[None, :]
    scores = jnp.where(self_mask[None], masked_score, scores)
    probs = jax.nn.softmax(scores, axis=-1)
    dprob = jnp.einsum("cqd,ckd->cqk", g_blocks, value_window, preferred_element_type=jnp.float32)
    dscore = probs * (dprob - jnp.sum(probs * dprob, axis=-1, keepdims=True))
    probs_low = probs.astype(jnp.bfloat16)
    dscore_low = dscore.astype(jnp.bfloat16)
    dquery = (
        jnp.einsum("cqk,ckd->cqd", dscore_low, key_window, preferred_element_type=jnp.float32)
        * scale_factor
    )
    dkey_window = (
        jnp.einsum("cqk,cqd->ckd", dscore_low, q_blocks, preferred_element_type=jnp.float32)
        * scale_factor
    )
    dvalue_window = jnp.einsum(
        "cqk,cqd->ckd", probs_low, g_blocks, preferred_element_type=jnp.float32
    )
    grad_window = jnp.concatenate([dkey_window, dvalue_window], axis=-1)
    own_part = grad_window[:, :GROUP]
    later_part = grad_window[1:, GROUP:]
    outgoing = grad_window[0, GROUP:]
    incoming = shifted(outgoing, SEQ, -1)
    key_value = (own_part + jnp.concatenate([later_part, incoming[None]], axis=0)).reshape(
        tok_count, 2 * head_width
    )
    dquery_s = dquery.reshape(tok_count, head_width)
    dkey_s = key_value[:, :head_width]
    dvalue_s = key_value[:, head_width:]
    query_float = sorted_query.astype(jnp.float32)
    norm_s = jnp.sqrt(jnp.sum(query_float * query_float, axis=1, keepdims=True) + eps_norm)
    along = jnp.sum(query_float * dkey_s, axis=1, keepdims=True)
    dshared_s = dquery_s + dkey_s / norm_s - query_float * (along / norm_s**3)
    sorted_grads = jnp.concatenate(
        [dshared_s.astype(jnp.bfloat16), dvalue_s.astype(jnp.bfloat16)], axis=1
    )
    nz, ny, nc = (lax.axis_size(a) for a in SEQ)
    my_core = lax.axis_index("c")
    slot_chip = recv_slots.reshape(peer_count // nc, nc, capacity)
    fanned = jnp.stack([jnp.roll(slot_chip, -j, axis=1) for j in range(nc)], axis=2).reshape(-1)
    to_fanned = (row_ids[:, None] == fanned[None, :]).astype(jnp.bfloat16)
    to_chip = (
        lax.dot_general(
            to_fanned, sorted_grads, (((0,), (0,)), ((), ())), preferred_element_type=jnp.float32
        )
        .astype(jnp.bfloat16)
        .reshape(peer_count, nc, capacity, 2 * head_width)
    )
    back_rows = lax.all_to_all(to_chip, SEQ, split_axis=0, concat_axis=0, tiled=True)
    rows = feat_count // (nz * ny * nc)
    blocks = whole.reshape(tok_count, nz, ny, nc, rows).transpose(3, 0, 1, 2, 4)
    shares = blocks.reshape(nc, tok_count, ny * nz * rows)
    index_block = jnp.zeros((tok_count, head_width), jnp.bfloat16).at[:, 0].set(
        buffer_index.astype(jnp.bfloat16)
    )
    outgoing_shares = jnp.concatenate(
        [shares, jnp.broadcast_to(index_block[None], (nc, tok_count, head_width))], axis=2
    )
    got_shares = []
    source_grads = []
    for j in range(nc):
        mine = jnp.take(outgoing_shares, (my_core + j) % nc, axis=0)
        got = mine if j == 0 else shifted(mine, "c", j)
        got_shares.append(got[:, : ny * nz * rows])
        rows_in = back_rows[:, (-j) % nc].reshape(peer_count * capacity, 2 * head_width)
        source_index = got[:, ny * nz * rows].astype(jnp.int32)
        source_buffer = (buffer_ids[:, None] == source_index[None, :]).astype(jnp.bfloat16)
        source_grads.append(
            lax.dot_general(
                source_buffer, rows_in, (((0,), (0,)), ((), ())), preferred_element_type=jnp.float32
            ).astype(jnp.bfloat16)
        )
    grads = lax.dot_general(
        jnp.concatenate(got_shares, axis=0),
        jnp.concatenate(source_grads, axis=0),
        (((0,), (0,)), ((), ())),
        preferred_element_type=jnp.float32,
    )
    grads = grads.reshape(nz * ny, rows, 2 * head_width)
    grads = jnp.sum(
        lax.all_to_all(grads.astype(jnp.bfloat16), ("z", "y"), 0, 0, tiled=True).astype(jnp.float32),
        axis=0,
    )
    grads = grads.reshape(rows, 2 * head_width)
    return (grads[:, :head_width], grads[:, head_width:])


def split_mesh(mesh):
    devices = mesh.devices
    seq_n, head_n = devices.shape
    column = devices[:, 0]
    cores = sorted({d.core_on_chip for d in column})
    ys = sorted({d.coords[1] for d in column})
    nc, ny = len(cores), len(ys)
    nz = seq_n // (nc * ny)
    grid = devices.reshape(nz, ny, nc, head_n)
    for z in range(nz):
        for y in range(ny):
            for c in range(nc):
                d = grid[z, y, c, 0]
                assert d.core_on_chip == cores[c] and d.coords[1] == ys[y]
    return Mesh(grid, SEQ + ("head",))


def solution(mesh):
    fine = split_mesh(mesh)
    in_specs = (
        P(SEQ, "head"),
        P(None, "head"),
        P(None, "head"),
        P(SEQ, "head"),
        P("head", SEQ),
    )
    out_specs = (P(SEQ, "head"), P(SEQ, "head"))
    return jax.shard_map(
        per_device, mesh=fine, in_specs=in_specs, out_specs=out_specs, check_vma=False
    )
```

```python
import math

import jax
import jax.numpy as jnp
from jax import lax
from jax.sharding import Mesh
from jax.sharding import PartitionSpec as P

GROUP = 64

SEQ = ("z", "y", "c")


eps_norm = 1e-06
masked_score = -1000000000.0


def shifted(value, axis, steps):
    count = lax.axis_size(axis)
    pairs = [(source, (source + steps) % count) for source in range(count)]
    return lax.ppermute(value, axis, pairs)


def unit_keys(block):
    block_float = block.astype(jnp.float32)
    norm_rows = jnp.sqrt(jnp.sum(block_float * block_float, axis=1, keepdims=True) + eps_norm)
    return (block_float / norm_rows).astype(jnp.bfloat16)


def per_device(tokens, shared_weight, value_weight, head_grad, sorted_slot):
    tok_count = tokens.shape[0]
    head_n = lax.axis_size("head")
    spread = jnp.broadcast_to(tokens[None], (head_n,) + tokens.shape)
    gathered = lax.all_to_all(spread, "head", 0, 0, tiled=True)
    whole = gathered.transpose(1, 0, 2).reshape(tok_count, head_n * tokens.shape[1])
    feat_count = whole.shape[1]
    head_width = shared_weight.shape[1]
    peer_count = lax.axis_size(SEQ)
    capacity = 2 * tok_count // peer_count
    group_count = tok_count // GROUP
    tail_start = tok_count - GROUP
    scale_factor = 1.0 / math.sqrt(head_width)
    query = jnp.dot(whole, shared_weight, preferred_element_type=jnp.float32).astype(jnp.bfloat16)
    values = jnp.dot(whole, value_weight, preferred_element_type=jnp.float32).astype(jnp.bfloat16)
    slot_ids = sorted_slot[0]
    target = slot_ids // tok_count
    local_slot = slot_ids - target * tok_count
    peer_ids = jnp.arange(peer_count, dtype=jnp.int32)
    row_ids = jnp.arange(tok_count, dtype=jnp.int32)
    earlier_rows = (row_ids[:, None] > row_ids[None, :]).astype(jnp.bfloat16)
    every_row = jnp.ones((tok_count,), dtype=bool)
    one_hot = ((target[:, None] == peer_ids[None, :]) & every_row[:, None]).astype(jnp.bfloat16)
    before = jnp.dot(earlier_rows, one_hot, preferred_element_type=jnp.float32)
    buffer_index = target * capacity + jnp.sum(before * one_hot.astype(jnp.float32), axis=1).astype(
        jnp.int32
    )
    is_tail = local_slot >= tail_start
    is_head = local_slot < GROUP

    def rank_within(mask):
        hot = one_hot * mask[:, None].astype(jnp.bfloat16)
        seen = jnp.dot(earlier_rows, hot, preferred_element_type=jnp.float32)
        return jnp.sum(seen * one_hot.astype(jnp.float32), axis=1).astype(jnp.int32)

    lanes = 3 * capacity
    slots = [
        target * lanes + buffer_index % capacity,
        ((target + 1) % peer_count) * lanes + capacity + rank_within(is_tail),
        ((target - 1) % peer_count) * lanes + 2 * capacity + rank_within(is_head),
    ]
    masks = [every_row, is_tail, is_head]
    window = 2 * GROUP + tok_count
    places = [local_slot + GROUP, local_slot - tail_start, local_slot + GROUP + tok_count]
    send_ids = jnp.arange(peer_count * lanes, dtype=jnp.int32)
    send_rows = jnp.zeros((peer_count * lanes, 4 * head_width), jnp.float32)
    used = jnp.zeros((peer_count * lanes,), jnp.float32)
    for slot, mask, place in zip(slots, masks, places):
        index_block = jnp.zeros((tok_count, head_width), jnp.bfloat16).at[:, 0].set(
            place.astype(jnp.bfloat16)
        )
        rows = jnp.concatenate([query, values, head_grad, index_block], axis=1)
        pick = ((send_ids[:, None] == slot[None, :]) & mask[None, :]).astype(jnp.bfloat16)
        send_rows = send_rows + jnp.dot(pick, rows, preferred_element_type=jnp.float32)
        used = used + jnp.sum(pick.astype(jnp.float32), axis=1)
    send_rows = send_rows.astype(jnp.bfloat16)
    empty = (send_ids[:, None] * 0 + jnp.arange(head_width)[None, :]) == 0
    send_rows = send_rows.at[:, 3 * head_width :].set(
        jnp.where(
            empty & (used[:, None] == 0),
            jnp.bfloat16(window),
            send_rows[:, 3 * head_width :],
        )
    )
    buffer_ids = jnp.arange(peer_count * capacity, dtype=jnp.int32)
    to_buffer = (buffer_ids[:, None] == buffer_index[None, :]).astype(jnp.bfloat16)
    recv_rows = lax.all_to_all(send_rows, SEQ, split_axis=0, concat_axis=0, tiled=True)
    recv_index = recv_rows[:, 3 * head_width].astype(jnp.int32)
    window_ids = jnp.arange(window, dtype=jnp.int32)
    to_window = (window_ids[:, None] == recv_index[None, :]).astype(jnp.bfloat16)
    window_rows = jnp.dot(
        to_window, recv_rows[:, : 3 * head_width], preferred_element_type=jnp.float32
    ).astype(jnp.bfloat16)
    recv_slots = recv_index.reshape(peer_count, lanes)[:, :capacity].reshape(-1) - GROUP
    to_sorted = (row_ids[:, None] == recv_slots[None, :]).astype(jnp.bfloat16)
    sorted_rows = window_rows[GROUP : GROUP + tok_count]
    sorted_query = sorted_rows[:, :head_width]
    span = group_count + 2
    all_q = window_rows[:, :head_width].reshape(span, GROUP, head_width)
    all_v = window_rows[:, head_width : 2 * head_width].reshape(span, GROUP, head_width)
    all_g = window_rows[:, 2 * head_width :].reshape(span, GROUP, head_width)
    all_k = unit_keys(window_rows[:, :head_width]).reshape(span, GROUP, head_width)
    q_blocks = all_q[1:]
    g_blocks = all_g[1:]
    key_window = jnp.concatenate([all_k[1:], all_k[:-1]], axis=1)
    value_window = jnp.concatenate([all_v[1:], all_v[:-1]], axis=1)
    scores = (
        jnp.einsum("cqd,ckd->cqk", q_blocks, key_window, preferred_element_type=jnp.float32)
        * scale_factor
    )
    self_mask = jnp.arange(GROUP)[:, None] == jnp.arange(2 * GROUP)[None, :]
    scores = jnp.where(self_mask[None], masked_score, scores)
    probs = jax.nn.softmax(scores, axis=-1)
    dprob = jnp.einsum("cqd,ckd->cqk", g_blocks, value_window, preferred_element_type=jnp.float32)
    dscore = probs * (dprob - jnp.sum(probs * dprob, axis=-1, keepdims=True))
    probs_low = probs.astype(jnp.bfloat16)
    dscore_low = dscore.astype(jnp.bfloat16)
    dquery = (
        jnp.einsum("cqk,ckd->cqd", dscore_low[:group_count], key_window[:group_count],
                   preferred_element_type=jnp.float32)
        * scale_factor
    )
    dkey_window = (
        jnp.einsum("cqk,cqd->ckd", dscore_low, q_blocks, preferred_element_type=jnp.float32)
        * scale_factor
    )
    dvalue_window = jnp.einsum(
        "cqk,cqd->ckd", probs_low, g_blocks, preferred_element_type=jnp.float32
    )
    grad_window = jnp.concatenate([dkey_window, dvalue_window], axis=-1)
    key_value = (grad_window[:group_count, :GROUP] + grad_window[1:, GROUP:]).reshape(
        tok_count, 2 * head_width
    )
    dquery_s = dquery.reshape(tok_count, head_width)
    dkey_s = key_value[:, :head_width]
    dvalue_s = key_value[:, head_width:]
    query_float = sorted_query.astype(jnp.float32)
    norm_s = jnp.sqrt(jnp.sum(query_float * query_float, axis=1, keepdims=True) + eps_norm)
    along = jnp.sum(query_float * dkey_s, axis=1, keepdims=True)
    dshared_s = dquery_s + dkey_s / norm_s - query_float * (along / norm_s**3)
    sorted_grads = jnp.concatenate(
        [dshared_s.astype(jnp.bfloat16), dvalue_s.astype(jnp.bfloat16)], axis=1
    )
    nz, ny, nc = (lax.axis_size(a) for a in SEQ)
    my_core = lax.axis_index("c")
    slot_chip = recv_slots.reshape(peer_count // nc, nc, capacity)
    fanned = jnp.stack([jnp.roll(slot_chip, -j, axis=1) for j in range(nc)], axis=2).reshape(-1)
    to_fanned = (row_ids[:, None] == fanned[None, :]).astype(jnp.bfloat16)
    to_chip = (
        lax.dot_general(
            to_fanned, sorted_grads, (((0,), (0,)), ((), ())), preferred_element_type=jnp.float32
        )
        .astype(jnp.bfloat16)
        .reshape(peer_count, nc, capacity, 2 * head_width)
    )
    back_rows = lax.all_to_all(to_chip, SEQ, split_axis=0, concat_axis=0, tiled=True)
    rows = feat_count // (nz * ny * nc)
    blocks = whole.reshape(tok_count, nz, ny, nc, rows).transpose(3, 0, 1, 2, 4)
    shares = blocks.reshape(nc, tok_count, ny * nz * rows)
    index_block = jnp.zeros((tok_count, head_width), jnp.bfloat16).at[:, 0].set(
        buffer_index.astype(jnp.bfloat16)
    )
    outgoing_shares = jnp.concatenate(
        [shares, jnp.broadcast_to(index_block[None], (nc, tok_count, head_width))], axis=2
    )
    got_shares = []
    source_grads = []
    for j in range(nc):
        mine = jnp.take(outgoing_shares, (my_core + j) % nc, axis=0)
        got = mine if j == 0 else shifted(mine, "c", j)
        got_shares.append(got[:, : ny * nz * rows])
        rows_in = back_rows[:, (-j) % nc].reshape(peer_count * capacity, 2 * head_width)
        source_index = got[:, ny * nz * rows].astype(jnp.int32)
        source_buffer = (buffer_ids[:, None] == source_index[None, :]).astype(jnp.bfloat16)
        source_grads.append(
            lax.dot_general(
                source_buffer, rows_in, (((0,), (0,)), ((), ())), preferred_element_type=jnp.float32
            ).astype(jnp.bfloat16)
        )
    grads = lax.dot_general(
        jnp.concatenate(got_shares, axis=0),
        jnp.concatenate(source_grads, axis=0),
        (((0,), (0,)), ((), ())),
        preferred_element_type=jnp.float32,
    )
    grads = grads.reshape(nz * ny, rows, 2 * head_width)
    grads = jnp.sum(
        lax.all_to_all(grads.astype(jnp.bfloat16), ("z", "y"), 0, 0, tiled=True).astype(jnp.float32),
        axis=0,
    )
    grads = grads.reshape(rows, 2 * head_width)
    return (grads[:, :head_width], grads[:, head_width:])


def split_mesh(mesh):
    devices = mesh.devices
    seq_n, head_n = devices.shape
    column = devices[:, 0]
    cores = sorted({d.core_on_chip for d in column})
    ys = sorted({d.coords[1] for d in column})
    nc, ny = len(cores), len(ys)
    nz = seq_n // (nc * ny)
    grid = devices.reshape(nz, ny, nc, head_n)
    for z in range(nz):
        for y in range(ny):
            for c in range(nc):
                d = grid[z, y, c, 0]
                assert d.core_on_chip == cores[c] and d.coords[1] == ys[y]
    return Mesh(grid, SEQ + ("head",))


def solution(mesh):
    fine = split_mesh(mesh)
    in_specs = (
        P(SEQ, "head"),
        P(None, "head"),
        P(None, "head"),
        P(SEQ, "head"),
        P("head", SEQ),
    )
    out_specs = (P(SEQ, "head"), P(SEQ, "head"))
    return jax.shard_map(
        per_device, mesh=fine, in_specs=in_specs, out_specs=out_specs, check_vma=False
    )
```

```python
import math

import jax
import jax.numpy as jnp
from jax import lax
from jax.sharding import Mesh
from jax.sharding import PartitionSpec as P

GROUP = 64

SEQ = ("z", "y", "c")


eps_norm = 1e-06
masked_score = -1000000000.0


def shifted(value, axis, steps):
    count = lax.axis_size(axis)
    pairs = [(source, (source + steps) % count) for source in range(count)]
    return lax.ppermute(value, axis, pairs)


def unit_keys(block):
    block_float = block.astype(jnp.float32)
    norm_rows = jnp.sqrt(jnp.sum(block_float * block_float, axis=1, keepdims=True) + eps_norm)
    return (block_float / norm_rows).astype(jnp.bfloat16)


def per_device(tokens, shared_weight, value_weight, head_grad, sorted_slot):
    tok_count = tokens.shape[0]
    head_n = lax.axis_size("head")
    spread = jnp.broadcast_to(tokens[None], (head_n,) + tokens.shape)
    gathered = lax.all_to_all(spread, "head", 0, 0, tiled=True)
    whole = gathered.transpose(1, 0, 2).reshape(tok_count, head_n * tokens.shape[1])
    feat_count = whole.shape[1]
    head_width = shared_weight.shape[1]
    peer_count = lax.axis_size(SEQ)
    capacity = 2 * tok_count // peer_count
    group_count = tok_count // GROUP
    tail_start = tok_count - GROUP
    scale_factor = 1.0 / math.sqrt(head_width)
    query = jnp.dot(whole, shared_weight, preferred_element_type=jnp.float32).astype(jnp.bfloat16)
    values = jnp.dot(whole, value_weight, preferred_element_type=jnp.float32).astype(jnp.bfloat16)
    slot_ids = sorted_slot[0]
    target = slot_ids // tok_count
    local_slot = slot_ids - target * tok_count
    peer_ids = jnp.arange(peer_count, dtype=jnp.int32)
    row_ids = jnp.arange(tok_count, dtype=jnp.int32)
    earlier_rows = (row_ids[:, None] > row_ids[None, :]).astype(jnp.bfloat16)
    every_row = jnp.ones((tok_count,), dtype=bool)
    one_hot = ((target[:, None] == peer_ids[None, :]) & every_row[:, None]).astype(jnp.bfloat16)
    before = jnp.dot(earlier_rows, one_hot, preferred_element_type=jnp.float32)
    buffer_index = target * capacity + jnp.sum(before * one_hot.astype(jnp.float32), axis=1).astype(
        jnp.int32
    )
    slot_block = jnp.zeros((tok_count, head_width), jnp.bfloat16).at[:, 0].set(
        local_slot.astype(jnp.bfloat16)
    )
    payload = jnp.concatenate([query, values, head_grad, slot_block], axis=1)
    buffer_ids = jnp.arange(peer_count * capacity, dtype=jnp.int32)
    to_buffer = (buffer_ids[:, None] == buffer_index[None, :]).astype(jnp.bfloat16)
    send_rows = jnp.dot(to_buffer, payload, preferred_element_type=jnp.float32).astype(jnp.bfloat16)
    empty = (buffer_ids[:, None] * 0 + jnp.arange(head_width)[None, :]) == 0
    used = jnp.sum(to_buffer.astype(jnp.float32), axis=1) > 0
    send_rows = send_rows.at[:, 3 * head_width :].set(
        jnp.where(
            empty & ~used[:, None],
            jnp.bfloat16(tok_count),
            send_rows[:, 3 * head_width :],
        )
    )
    recv_rows = lax.all_to_all(send_rows, SEQ, split_axis=0, concat_axis=0, tiled=True)
    recv_slots = recv_rows[:, 3 * head_width].astype(jnp.int32)
    to_sorted = (row_ids[:, None] == recv_slots[None, :]).astype(jnp.bfloat16)
    sorted_rows = jnp.dot(
        to_sorted, recv_rows[:, : 3 * head_width], preferred_element_type=jnp.float32
    ).astype(jnp.bfloat16)
    halo_rows = shifted(sorted_rows[tail_start:, : 2 * head_width], SEQ, 1)
    sorted_query = sorted_rows[:, :head_width]
    own_keys = unit_keys(sorted_query).reshape(group_count, GROUP, head_width)
    halo_keys = unit_keys(halo_rows[:, :head_width])
    q_blocks = sorted_query.reshape(group_count, GROUP, head_width)
    v_blocks = sorted_rows[:, head_width : 2 * head_width].reshape(group_count, GROUP, head_width)
    g_blocks = sorted_rows[:, 2 * head_width :].reshape(group_count, GROUP, head_width)
    prev_keys = jnp.concatenate([halo_keys[None], own_keys[:-1]], axis=0)
    prev_values = jnp.concatenate([halo_rows[None, :, head_width:], v_blocks[:-1]], axis=0)
    key_window = jnp.concatenate([own_keys, prev_keys], axis=1)
    value_window = jnp.concatenate([v_blocks, prev_values], axis=1)
    scores = (
        jnp.einsum("cqd,ckd->cqk", q_blocks, key_window, preferred_element_type=jnp.float32)
        * scale_factor
    )
    self_mask = jnp.arange(GROUP)[:, None] == jnp.arange(2 * GROUP)[None, :]
    scores = jnp.where(self_mask[None], masked_score, scores)
    probs = jax.nn.softmax(scores, axis=-1)
    dprob = jnp.einsum("cqd,ckd->cqk", g_blocks, value_window, preferred_element_type=jnp.float32)
    dscore = probs * (dprob - jnp.sum(probs * dprob, axis=-1, keepdims=True))
    probs_low = probs.astype(jnp.bfloat16)
    dscore_low = dscore.astype(jnp.bfloat16)
    dquery = (
        jnp.einsum("cqk,ckd->cqd", dscore_low, key_window, preferred_element_type=jnp.float32)
        * scale_factor
    )
    dkey_window = (
        jnp.einsum("cqk,cqd->ckd", dscore_low, q_blocks, preferred_element_type=jnp.float32)
        * scale_factor
    )
    dvalue_window = jnp.einsum(
        "cqk,cqd->ckd", probs_low, g_blocks, preferred_element_type=jnp.float32
    )
    grad_window = jnp.concatenate([dkey_window, dvalue_window], axis=-1)
    own_part = grad_window[:, :GROUP]
    later_part = grad_window[1:, GROUP:]
    outgoing = grad_window[0, GROUP:]
    incoming = shifted(outgoing, SEQ, -1)
    key_value = (own_part + jnp.concatenate([later_part, incoming[None]], axis=0)).reshape(
        tok_count, 2 * head_width
    )
    dquery_s = dquery.reshape(tok_count, head_width)
    dkey_s = key_value[:, :head_width]
    dvalue_s = key_value[:, head_width:]
    query_float = sorted_query.astype(jnp.float32)
    norm_s = jnp.sqrt(jnp.sum(query_float * query_float, axis=1, keepdims=True) + eps_norm)
    along = jnp.sum(query_float * dkey_s, axis=1, keepdims=True)
    dshared_s = dquery_s + dkey_s / norm_s - query_float * (along / norm_s**3)
    sorted_grads = jnp.concatenate(
        [dshared_s.astype(jnp.bfloat16), dvalue_s.astype(jnp.bfloat16)], axis=1
    )
    nz, ny, nc = (lax.axis_size(a) for a in SEQ)
    my_core = lax.axis_index("c")
    slot_chip = recv_slots.reshape(peer_count // nc, nc, capacity)
    fanned = jnp.stack([jnp.roll(slot_chip, -j, axis=1) for j in range(nc)], axis=2).reshape(-1)
    to_fanned = (row_ids[:, None] == fanned[None, :]).astype(jnp.bfloat16)
    to_chip = (
        lax.dot_general(
            to_fanned, sorted_grads, (((0,), (0,)), ((), ())), preferred_element_type=jnp.float32
        )
        .astype(jnp.bfloat16)
        .reshape(peer_count, nc, capacity, 2 * head_width)
    )
    back_rows = lax.all_to_all(to_chip, SEQ, split_axis=0, concat_axis=0, tiled=True)
    rows = feat_count // (nz * ny * nc)
    blocks = whole.reshape(tok_count, nz, ny, nc, rows).transpose(3, 0, 2, 1, 4)
    shares = blocks.reshape(nc, tok_count, ny * nz * rows)
    index_block = jnp.zeros((tok_count, head_width), jnp.bfloat16).at[:, 0].set(
        buffer_index.astype(jnp.bfloat16)
    )
    outgoing_shares = jnp.concatenate(
        [shares, jnp.broadcast_to(index_block[None], (nc, tok_count, head_width))], axis=2
    )
    got_shares = []
    source_grads = []
    for j in range(nc):
        mine = jnp.take(outgoing_shares, (my_core + j) % nc, axis=0)
        got = mine if j == 0 else shifted(mine, "c", j)
        got_shares.append(got[:, : ny * nz * rows])
        rows_in = back_rows[:, (-j) % nc].reshape(peer_count * capacity, 2 * head_width)
        source_index = got[:, ny * nz * rows].astype(jnp.int32)
        source_buffer = (buffer_ids[:, None] == source_index[None, :]).astype(jnp.bfloat16)
        source_grads.append(
            lax.dot_general(
                source_buffer, rows_in, (((0,), (0,)), ((), ())), preferred_element_type=jnp.float32
            ).astype(jnp.bfloat16)
        )
    grads = lax.dot_general(
        jnp.concatenate(got_shares, axis=0),
        jnp.concatenate(source_grads, axis=0),
        (((0,), (0,)), ((), ())),
        preferred_element_type=jnp.float32,
    )
    grads = grads.reshape(ny * nz, rows, 2 * head_width)
    grads = jnp.sum(
        lax.all_to_all(grads.astype(jnp.bfloat16), ("y", "z"), 0, 0, tiled=True).astype(jnp.float32),
        axis=0,
    )
    grads = grads.reshape(rows, 2 * head_width)
    return (grads[:, :head_width], grads[:, head_width:])


def split_mesh(mesh):
    devices = mesh.devices
    seq_n, head_n = devices.shape
    column = devices[:, 0]
    cores = sorted({d.core_on_chip for d in column})
    ys = sorted({d.coords[1] for d in column})
    nc, ny = len(cores), len(ys)
    nz = seq_n // (nc * ny)
    grid = devices.reshape(nz, ny, nc, head_n)
    for z in range(nz):
        for y in range(ny):
            for c in range(nc):
                d = grid[z, y, c, 0]
                assert d.core_on_chip == cores[c] and d.coords[1] == ys[y]
    return Mesh(grid, SEQ + ("head",))


def solution(mesh):
    fine = split_mesh(mesh)
    in_specs = (
        P(SEQ, "head"),
        P(None, "head"),
        P(None, "head"),
        P(SEQ, "head"),
        P("head", SEQ),
    )
    out_specs = (P(SEQ, "head"), P(SEQ, "head"))
    return jax.shard_map(
        per_device, mesh=fine, in_specs=in_specs, out_specs=out_specs, check_vma=False
    )
```

```python
import math

import jax
import jax.numpy as jnp
from jax import lax
from jax.sharding import Mesh
from jax.sharding import PartitionSpec as P

GROUP = 64

SEQ = ("z", "y", "c")


eps_norm = 1e-06
masked_score = -1000000000.0


def shifted(value, axis, steps):
    count = lax.axis_size(axis)
    pairs = [(source, (source + steps) % count) for source in range(count)]
    return lax.ppermute(value, axis, pairs)


def unit_keys(block):
    block_float = block.astype(jnp.float32)
    norm_rows = jnp.sqrt(jnp.sum(block_float * block_float, axis=1, keepdims=True) + eps_norm)
    return (block_float / norm_rows).astype(jnp.bfloat16)


def per_device(tokens, shared_weight, value_weight, head_grad, sorted_slot):
    tok_count = tokens.shape[0]
    head_n = lax.axis_size("head")
    spread = jnp.broadcast_to(tokens[None], (head_n,) + tokens.shape)
    gathered = lax.all_to_all(spread, "head", 0, 0, tiled=True)
    whole = gathered.transpose(1, 0, 2).reshape(tok_count, head_n * tokens.shape[1])
    feat_count = whole.shape[1]
    head_width = shared_weight.shape[1]
    peer_count = lax.axis_size(SEQ)
    capacity = 2 * tok_count // peer_count
    group_count = tok_count // GROUP
    tail_start = tok_count - GROUP
    scale_factor = 1.0 / math.sqrt(head_width)
    query = jnp.dot(whole, shared_weight, preferred_element_type=jnp.float32).astype(jnp.bfloat16)
    values = jnp.dot(whole, value_weight, preferred_element_type=jnp.float32).astype(jnp.bfloat16)
    slot_ids = sorted_slot[0]
    target = slot_ids // tok_count
    local_slot = slot_ids - target * tok_count
    peer_ids = jnp.arange(peer_count, dtype=jnp.int32)
    row_ids = jnp.arange(tok_count, dtype=jnp.int32)
    earlier_rows = (row_ids[:, None] > row_ids[None, :]).astype(jnp.bfloat16)
    every_row = jnp.ones((tok_count,), dtype=bool)
    one_hot = ((target[:, None] == peer_ids[None, :]) & every_row[:, None]).astype(jnp.bfloat16)
    before = jnp.dot(earlier_rows, one_hot, preferred_element_type=jnp.float32)
    buffer_index = target * capacity + jnp.sum(before * one_hot.astype(jnp.float32), axis=1).astype(
        jnp.int32
    )
    slot_block = jnp.zeros((tok_count, head_width), jnp.bfloat16).at[:, 0].set(
        (local_slot + 1).astype(jnp.bfloat16)
    )
    payload = jnp.concatenate([query, values, head_grad, slot_block], axis=1)
    buffer_ids = jnp.arange(peer_count * capacity, dtype=jnp.int32)
    to_buffer = (buffer_ids[:, None] == buffer_index[None, :]).astype(jnp.bfloat16)
    send_rows = jnp.dot(to_buffer, payload, preferred_element_type=jnp.float32).astype(jnp.bfloat16)
    recv_rows = lax.all_to_all(send_rows, SEQ, split_axis=0, concat_axis=0, tiled=True)
    recv_slots = recv_rows[:, 3 * head_width].astype(jnp.int32) - 1
    to_sorted = (row_ids[:, None] == recv_slots[None, :]).astype(jnp.bfloat16)
    sorted_rows = jnp.dot(
        to_sorted, recv_rows[:, : 3 * head_width], preferred_element_type=jnp.float32
    ).astype(jnp.bfloat16)
    halo_rows = shifted(sorted_rows[tail_start:, : 2 * head_width], SEQ, 1)
    sorted_query = sorted_rows[:, :head_width]
    own_keys = unit_keys(sorted_query).reshape(group_count, GROUP, head_width)
    halo_keys = unit_keys(halo_rows[:, :head_width])
    q_blocks = sorted_query.reshape(group_count, GROUP, head_width)
    v_blocks = sorted_rows[:, head_width : 2 * head_width].reshape(group_count, GROUP, head_width)
    g_blocks = sorted_rows[:, 2 * head_width :].reshape(group_count, GROUP, head_width)
    prev_keys = jnp.concatenate([halo_keys[None], own_keys[:-1]], axis=0)
    prev_values = jnp.concatenate([halo_rows[None, :, head_width:], v_blocks[:-1]], axis=0)
    key_window = jnp.concatenate([own_keys, prev_keys], axis=1)
    value_window = jnp.concatenate([v_blocks, prev_values], axis=1)
    scores = (
        jnp.einsum("cqd,ckd->cqk", q_blocks, key_window, preferred_element_type=jnp.float32)
        * scale_factor
    )
    self_mask = jnp.arange(GROUP)[:, None] == jnp.arange(2 * GROUP)[None, :]
    scores = jnp.where(self_mask[None], masked_score, scores)
    probs = jax.nn.softmax(scores, axis=-1)
    dprob = jnp.einsum("cqd,ckd->cqk", g_blocks, value_window, preferred_element_type=jnp.float32)
    dscore = probs * (dprob - jnp.sum(probs * dprob, axis=-1, keepdims=True))
    probs_low = probs.astype(jnp.bfloat16)
    dscore_low = dscore.astype(jnp.bfloat16)
    dquery = (
        jnp.einsum("cqk,ckd->cqd", dscore_low, key_window, preferred_element_type=jnp.float32)
        * scale_factor
    )
    dkey_window = (
        jnp.einsum("cqk,cqd->ckd", dscore_low, q_blocks, preferred_element_type=jnp.float32)
        * scale_factor
    )
    dvalue_window = jnp.einsum(
        "cqk,cqd->ckd", probs_low, g_blocks, preferred_element_type=jnp.float32
    )
    grad_window = jnp.concatenate([dkey_window, dvalue_window], axis=-1)
    own_part = grad_window[:, :GROUP]
    later_part = grad_window[1:, GROUP:]
    outgoing = grad_window[0, GROUP:]
    incoming = shifted(outgoing, SEQ, -1)
    key_value = (own_part + jnp.concatenate([later_part, incoming[None]], axis=0)).reshape(
        tok_count, 2 * head_width
    )
    dquery_s = dquery.reshape(tok_count, head_width)
    dkey_s = key_value[:, :head_width]
    dvalue_s = key_value[:, head_width:]
    query_float = sorted_query.astype(jnp.float32)
    norm_s = jnp.sqrt(jnp.sum(query_float * query_float, axis=1, keepdims=True) + eps_norm)
    along = jnp.sum(query_float * dkey_s, axis=1, keepdims=True)
    dshared_s = dquery_s + dkey_s / norm_s - query_float * (along / norm_s**3)
    sorted_grads = jnp.concatenate(
        [dshared_s.astype(jnp.bfloat16), dvalue_s.astype(jnp.bfloat16)], axis=1
    )
    nz, ny, nc = (lax.axis_size(a) for a in SEQ)
    my_core = lax.axis_index("c")
    slot_chip = recv_slots.reshape(peer_count // nc, nc, capacity)
    fanned = jnp.stack([jnp.roll(slot_chip, -j, axis=1) for j in range(nc)], axis=2).reshape(-1)
    to_fanned = (row_ids[:, None] == fanned[None, :]).astype(jnp.bfloat16)
    to_chip = (
        lax.dot_general(
            to_fanned, sorted_grads, (((0,), (0,)), ((), ())), preferred_element_type=jnp.float32
        )
        .astype(jnp.bfloat16)
        .reshape(peer_count, nc, capacity, 2 * head_width)
    )
    back_rows = lax.all_to_all(to_chip, SEQ, split_axis=0, concat_axis=0, tiled=True)
    rows = feat_count // (nz * ny * nc)
    blocks = whole.reshape(tok_count, nz, ny, nc, rows).transpose(3, 0, 1, 2, 4)
    shares = blocks.reshape(nc, tok_count, ny * nz * rows)
    index_block = jnp.zeros((tok_count, head_width), jnp.bfloat16).at[:, 0].set(
        buffer_index.astype(jnp.bfloat16)
    )
    outgoing_shares = jnp.concatenate(
        [shares, jnp.broadcast_to(index_block[None], (nc, tok_count, head_width))], axis=2
    )
    got_shares = []
    source_grads = []
    for j in range(nc):
        mine = jnp.take(outgoing_shares, (my_core + j) % nc, axis=0)
        got = mine if j == 0 else shifted(mine, "c", j)
        got_shares.append(got[:, : ny * nz * rows])
        rows_in = back_rows[:, (-j) % nc].reshape(peer_count * capacity, 2 * head_width)
        source_index = got[:, ny * nz * rows].astype(jnp.int32)
        source_buffer = (buffer_ids[:, None] == source_index[None, :]).astype(jnp.bfloat16)
        source_grads.append(
            lax.dot_general(
                source_buffer, rows_in, (((0,), (0,)), ((), ())), preferred_element_type=jnp.float32
            ).astype(jnp.bfloat16)
        )
    grads = lax.dot_general(
        jnp.concatenate(got_shares, axis=0),
        jnp.concatenate(source_grads, axis=0),
        (((0,), (0,)), ((), ())),
        preferred_element_type=jnp.float32,
    )
    grads = grads.reshape(nz * ny, rows, 2 * head_width)
    grads = jnp.sum(
        lax.all_to_all(grads.astype(jnp.bfloat16), ("z", "y"), 0, 0, tiled=True).astype(jnp.float32),
        axis=0,
    )
    grads = grads.reshape(rows, 2 * head_width)
    return (grads[:, :head_width], grads[:, head_width:])


def split_mesh(mesh):
    devices = mesh.devices
    seq_n, head_n = devices.shape
    column = devices[:, 0]
    cores = sorted({d.core_on_chip for d in column})
    ys = sorted({d.coords[1] for d in column})
    nc, ny = len(cores), len(ys)
    nz = seq_n // (nc * ny)
    grid = devices.reshape(nz, ny, nc, head_n)
    for z in range(nz):
        for y in range(ny):
            for c in range(nc):
                d = grid[z, y, c, 0]
                assert d.core_on_chip == cores[c] and d.coords[1] == ys[y]
    return Mesh(grid, SEQ + ("head",))


def solution(mesh):
    fine = split_mesh(mesh)
    in_specs = (
        P(SEQ, "head"),
        P(None, "head"),
        P(None, "head"),
        P(SEQ, "head"),
        P("head", SEQ),
    )
    out_specs = (P(SEQ, "head"), P(SEQ, "head"))
    return jax.shard_map(
        per_device, mesh=fine, in_specs=in_specs, out_specs=out_specs, check_vma=False
    )
```

```python
import math

import jax
import jax.numpy as jnp
from jax import lax
from jax.sharding import Mesh
from jax.sharding import PartitionSpec as P

GROUP = 64

SEQ = ("z", "y", "c")


eps_norm = 1e-06
masked_score = -1000000000.0


def shifted(value, axis, steps):
    count = lax.axis_size(axis)
    pairs = [(source, (source + steps) % count) for source in range(count)]
    return lax.ppermute(value, axis, pairs)


def unit_keys(block):
    block_float = block.astype(jnp.float32)
    norm_rows = jnp.sqrt(jnp.sum(block_float * block_float, axis=1, keepdims=True) + eps_norm)
    return (block_float / norm_rows).astype(jnp.bfloat16)


def per_device(tokens, shared_weight, value_weight, head_grad, sorted_slot):
    tok_count = tokens.shape[0]
    head_n = lax.axis_size("head")
    spread = jnp.broadcast_to(tokens[None], (head_n,) + tokens.shape)
    gathered = lax.all_to_all(spread, "head", 0, 0, tiled=True)
    whole = gathered.transpose(1, 0, 2).reshape(tok_count, head_n * tokens.shape[1])
    feat_count = whole.shape[1]
    head_width = shared_weight.shape[1]
    peer_count = lax.axis_size(SEQ)
    capacity = 2 * tok_count // peer_count
    group_count = tok_count // GROUP
    tail_start = tok_count - GROUP
    scale_factor = 1.0 / math.sqrt(head_width)
    both = jnp.dot(
        whole,
        jnp.concatenate([shared_weight, value_weight], axis=1),
        preferred_element_type=jnp.float32,
    ).astype(jnp.bfloat16)
    query = both[:, :head_width]
    values = both[:, head_width:]
    slot_ids = sorted_slot[0]
    target = slot_ids // tok_count
    local_slot = slot_ids - target * tok_count
    peer_ids = jnp.arange(peer_count, dtype=jnp.int32)
    row_ids = jnp.arange(tok_count, dtype=jnp.int32)
    earlier_rows = (row_ids[:, None] > row_ids[None, :]).astype(jnp.bfloat16)
    every_row = jnp.ones((tok_count,), dtype=bool)
    one_hot = ((target[:, None] == peer_ids[None, :]) & every_row[:, None]).astype(jnp.bfloat16)
    before = jnp.dot(earlier_rows, one_hot, preferred_element_type=jnp.float32)
    buffer_index = target * capacity + jnp.sum(before * one_hot.astype(jnp.float32), axis=1).astype(
        jnp.int32
    )
    slot_block = jnp.zeros((tok_count, head_width), jnp.bfloat16).at[:, 0].set(
        (local_slot + 1).astype(jnp.bfloat16)
    )
    payload = jnp.concatenate([query, values, head_grad, slot_block], axis=1)
    buffer_ids = jnp.arange(peer_count * capacity, dtype=jnp.int32)
    to_buffer = (buffer_ids[:, None] == buffer_index[None, :]).astype(jnp.bfloat16)
    send_rows = jnp.dot(to_buffer, payload, preferred_element_type=jnp.float32).astype(jnp.bfloat16)
    recv_rows = lax.all_to_all(send_rows, SEQ, split_axis=0, concat_axis=0, tiled=True)
    recv_slots = recv_rows[:, 3 * head_width].astype(jnp.int32) - 1
    to_sorted = (row_ids[:, None] == recv_slots[None, :]).astype(jnp.bfloat16)
    sorted_rows = jnp.dot(
        to_sorted, recv_rows[:, : 3 * head_width], preferred_element_type=jnp.float32
    ).astype(jnp.bfloat16)
    halo_rows = shifted(sorted_rows[tail_start:, : 2 * head_width], SEQ, 1)
    sorted_query = sorted_rows[:, :head_width]
    own_keys = unit_keys(sorted_query).reshape(group_count, GROUP, head_width)
    halo_keys = unit_keys(halo_rows[:, :head_width])
    q_blocks = sorted_query.reshape(group_count, GROUP, head_width)
    v_blocks = sorted_rows[:, head_width : 2 * head_width].reshape(group_count, GROUP, head_width)
    g_blocks = sorted_rows[:, 2 * head_width :].reshape(group_count, GROUP, head_width)
    prev_keys = jnp.concatenate([halo_keys[None], own_keys[:-1]], axis=0)
    prev_values = jnp.concatenate([halo_rows[None, :, head_width:], v_blocks[:-1]], axis=0)
    key_window = jnp.concatenate([own_keys, prev_keys], axis=1)
    value_window = jnp.concatenate([v_blocks, prev_values], axis=1)
    scores = (
        jnp.einsum("cqd,ckd->cqk", q_blocks, key_window, preferred_element_type=jnp.float32)
        * scale_factor
    )
    self_mask = jnp.arange(GROUP)[:, None] == jnp.arange(2 * GROUP)[None, :]
    scores = jnp.where(self_mask[None], masked_score, scores)
    probs = jax.nn.softmax(scores, axis=-1)
    dprob = jnp.einsum("cqd,ckd->cqk", g_blocks, value_window, preferred_element_type=jnp.float32)
    dscore = probs * (dprob - jnp.sum(probs * dprob, axis=-1, keepdims=True))
    probs_low = probs.astype(jnp.bfloat16)
    dscore_low = dscore.astype(jnp.bfloat16)
    dquery = (
        jnp.einsum("cqk,ckd->cqd", dscore_low, key_window, preferred_element_type=jnp.float32)
        * scale_factor
    )
    dkey_window = (
        jnp.einsum("cqk,cqd->ckd", dscore_low, q_blocks, preferred_element_type=jnp.float32)
        * scale_factor
    )
    dvalue_window = jnp.einsum(
        "cqk,cqd->ckd", probs_low, g_blocks, preferred_element_type=jnp.float32
    )
    grad_window = jnp.concatenate([dkey_window, dvalue_window], axis=-1)
    own_part = grad_window[:, :GROUP]
    later_part = grad_window[1:, GROUP:]
    outgoing = grad_window[0, GROUP:]
    incoming = shifted(outgoing, SEQ, -1)
    key_value = (own_part + jnp.concatenate([later_part, incoming[None]], axis=0)).reshape(
        tok_count, 2 * head_width
    )
    dquery_s = dquery.reshape(tok_count, head_width)
    dkey_s = key_value[:, :head_width]
    dvalue_s = key_value[:, head_width:]
    query_float = sorted_query.astype(jnp.float32)
    norm_s = jnp.sqrt(jnp.sum(query_float * query_float, axis=1, keepdims=True) + eps_norm)
    along = jnp.sum(query_float * dkey_s, axis=1, keepdims=True)
    dshared_s = dquery_s + dkey_s / norm_s - query_float * (along / norm_s**3)
    sorted_grads = jnp.concatenate(
        [dshared_s.astype(jnp.bfloat16), dvalue_s.astype(jnp.bfloat16)], axis=1
    )
    nz, ny, nc = (lax.axis_size(a) for a in SEQ)
    my_core = lax.axis_index("c")
    slot_chip = recv_slots.reshape(peer_count // nc, nc, capacity)
    fanned = jnp.stack([jnp.roll(slot_chip, -j, axis=1) for j in range(nc)], axis=2).reshape(-1)
    to_fanned = (row_ids[:, None] == fanned[None, :]).astype(jnp.bfloat16)
    to_chip = (
        lax.dot_general(
            to_fanned, sorted_grads, (((0,), (0,)), ((), ())), preferred_element_type=jnp.float32
        )
        .astype(jnp.bfloat16)
        .reshape(peer_count, nc, capacity, 2 * head_width)
    )
    back_rows = lax.all_to_all(to_chip, SEQ, split_axis=0, concat_axis=0, tiled=True)
    rows = feat_count // (nz * ny * nc)
    blocks = whole.reshape(tok_count, nz, ny, nc, rows).transpose(3, 0, 1, 2, 4)
    shares = blocks.reshape(nc, tok_count, ny * nz * rows)
    index_block = jnp.zeros((tok_count, head_width), jnp.bfloat16).at[:, 0].set(
        buffer_index.astype(jnp.bfloat16)
    )
    outgoing_shares = jnp.concatenate(
        [shares, jnp.broadcast_to(index_block[None], (nc, tok_count, head_width))], axis=2
    )
    got_shares = []
    source_grads = []
    for j in range(nc):
        mine = jnp.take(outgoing_shares, (my_core + j) % nc, axis=0)
        got = mine if j == 0 else shifted(mine, "c", j)
        got_shares.append(got[:, : ny * nz * rows])
        rows_in = back_rows[:, (-j) % nc].reshape(peer_count * capacity, 2 * head_width)
        source_index = got[:, ny * nz * rows].astype(jnp.int32)
        source_buffer = (buffer_ids[:, None] == source_index[None, :]).astype(jnp.bfloat16)
        source_grads.append(
            lax.dot_general(
                source_buffer, rows_in, (((0,), (0,)), ((), ())), preferred_element_type=jnp.float32
            ).astype(jnp.bfloat16)
        )
    grads = lax.dot_general(
        jnp.concatenate(got_shares, axis=0),
        jnp.concatenate(source_grads, axis=0),
        (((0,), (0,)), ((), ())),
        preferred_element_type=jnp.float32,
    )
    grads = grads.reshape(nz * ny, rows, 2 * head_width)
    grads = jnp.sum(
        lax.all_to_all(grads.astype(jnp.bfloat16), ("z", "y"), 0, 0, tiled=True).astype(jnp.float32),
        axis=0,
    )
    grads = grads.reshape(rows, 2 * head_width)
    return (grads[:, :head_width], grads[:, head_width:])


def split_mesh(mesh):
    devices = mesh.devices
    seq_n, head_n = devices.shape
    column = devices[:, 0]
    cores = sorted({d.core_on_chip for d in column})
    ys = sorted({d.coords[1] for d in column})
    nc, ny = len(cores), len(ys)
    nz = seq_n // (nc * ny)
    grid = devices.reshape(nz, ny, nc, head_n)
    for z in range(nz):
        for y in range(ny):
            for c in range(nc):
                d = grid[z, y, c, 0]
                assert d.core_on_chip == cores[c] and d.coords[1] == ys[y]
    return Mesh(grid, SEQ + ("head",))


def solution(mesh):
    fine = split_mesh(mesh)
    in_specs = (
        P(SEQ, "head"),
        P(None, "head"),
        P(None, "head"),
        P(SEQ, "head"),
        P("head", SEQ),
    )
    out_specs = (P(SEQ, "head"), P(SEQ, "head"))
    return jax.shard_map(
        per_device, mesh=fine, in_specs=in_specs, out_specs=out_specs, check_vma=False
    )
```
